128 devices in a mesh: dp: 8 (over x_hi, z), lm: 16 (over y, x_lo, core).
Axes of the slice: x: 4 (x_hi: 2, x_lo: 2; x = x_hi * 2 + x_lo), y: 4, z: 4, core: 2. Of those that a mesh axis runs over, the one named last changes fastest.
Arguments:
- queries: bfloat16 [16384, 256], P('dp', 'lm'), may hold values from -6 to 6
- landmarks: bfloat16 [65536, 256], P('lm'), may hold values from -6 to 6
- targets: bfloat16 [16384, 64], P('dp'), may hold values from -6 to 6
- ridge: float32 [64], replicated, may hold values from 4 to 64
Outputs:
- fit: float32 [16384, 64], P('dp')
The draws below stay inside these ranges and needn't reach their ends.
All inputs are finite; a program needn't handle non-finite values.
Results may differ from the reference program's by a relative error of at most 0.0006.
The reference program's roundings to bfloat16 on the way (of `qhat`, `chat` and `kernel`) count: a program that leaves them out, or rounds other values in their place, can miss the bound.
Values may be sent and summed in bfloat16 or wider, within the bound.
No kernel may reach another device: no remote copies, remote signals or barrier semaphores. Data moves between devices by JAX's collectives and lax.ppermute only.
A program may use at most 128 MiB of HBM per device.

```python
import math
import jax
import jax.numpy as jnp
from jax import lax

D = 256
TARGETS = 64
LM_DEV = 4096
ITERS = 2
QUERIES = 16384
LANDMARKS = 65536
N_LM = 16


def levels(key, dims, cuts, low, top_value):
    level = 1.0
    for dim, shards_of in cuts:
        heights = jax.random.uniform(jax.random.fold_in(jax.random.fold_in(key, 6), dim), (shards_of,), jnp.float32, low / len(cuts), top_value / len(cuts))
        level = level * jnp.repeat(jnp.exp(heights), dims[dim] // shards_of).reshape((-1,) + (1,) * (len(dims) - 1 - dim))
    return level


def bell_draw(stream_key, dims, width, bound, split=(), dtype=jnp.bfloat16):
    result = width * jax.random.normal(stream_key, dims, jnp.float32)
    if split:
        result = result * levels(stream_key, dims, split, -0.22, 0.18)
    return jnp.clip(result, -bound, bound).astype(dtype)


def setup_inputs(seed: int = 0) -> dict:
    keys = jax.random.split(jax.random.key(seed), 5)
    queries = bell_draw(keys[0], (QUERIES, D), 1.0, 6.0, ((0, 8), (1, 16)))
    landmarks = bell_draw(keys[1], (LANDMARKS, D), 1.0, 6.0, ((0, 16),))
    targets = bell_draw(keys[2], (QUERIES, TARGETS), 1.0, 6.0, ((0, 8),))
    ridge = jnp.clip(jnp.exp(jax.random.uniform(keys[3], (TARGETS,), jnp.float32, math.log(4.0), math.log(64.0))), 4.0, 64.0)
    return dict(queries=queries, landmarks=landmarks, targets=targets, ridge=ridge)


sharpness = 8.0
epsilon = 1e-06

def normalize(rows):
    values = rows.astype(jnp.float32)
    scale = lax.rsqrt(lax.optimization_barrier(jnp.sum(values * values, axis=1, keepdims=True)) + epsilon)
    return (values * scale).astype(jnp.bfloat16)

def reference(queries, landmarks, targets, ridge):
    qhat = normalize(queries)
    chat = normalize(landmarks).reshape(N_LM, LM_DEV, D)

    def tile(block):
        scores = jnp.dot(qhat, block.T, preferred_element_type=jnp.float32)
        return jnp.exp(2.0 * sharpness * scores).astype(jnp.bfloat16)
    kernel = lax.map(tile, chat)

    def left(vec_bf):
        pieces = vec_bf.reshape(N_LM, LM_DEV, TARGETS)

        def add_block(total, item):
            block, piece = item
            return (total + jnp.dot(block, piece, preferred_element_type=jnp.float32), None)
        total, unused = lax.scan(add_block, jnp.zeros((QUERIES, TARGETS), jnp.float32), (kernel, pieces))
        return total

    def right(rows_bf):

        def one(block):
            return lax.dot_general(block, rows_bf, (((0,), (0,)), ((), ())), preferred_element_type=jnp.float32)
        return lax.map(one, kernel).reshape(LANDMARKS, -1)

    def squares(block):
        values = block.astype(jnp.float32)
        return lax.optimization_barrier(jnp.sum(values * values, axis=0))
    rhs = right(targets) / QUERIES
    precond = lax.map(squares, kernel).reshape(LANDMARKS)[:, None] / QUERIES + ridge[None, :]
    coefficients = jnp.zeros((LANDMARKS, TARGETS), jnp.float32)
    residual = rhs
    direction = residual / precond
    norm_now = lax.optimization_barrier(jnp.sum(residual * residual / precond, axis=0))
    for step in range(ITERS):
        query_image = left(direction.astype(jnp.bfloat16)).astype(jnp.bfloat16)
        image = right(query_image) / QUERIES + ridge[None, :] * direction
        alpha = norm_now / lax.optimization_barrier(jnp.sum(direction * image, axis=0))
        coefficients = coefficients + alpha[None, :] * direction
        residual = residual - alpha[None, :] * image
        if step + 1 < ITERS:
            norm_next = lax.optimization_barrier(jnp.sum(residual * residual / precond, axis=0))
            direction = residual / precond + (norm_next / norm_now)[None, :] * direction
            norm_now = norm_next
    return left(coefficients.astype(jnp.bfloat16))
```

```python
import jax
import jax.numpy as jnp
from jax import lax
from jax.sharding import PartitionSpec as P

ITERS = 2


sharpness = 8.0
epsilon = 1e-06


def normalize(rows):
    values = rows.astype(jnp.float32)
    scale = lax.rsqrt(jnp.sum(values * values, axis=1, keepdims=True) + epsilon)
    return (values * scale).astype(jnp.bfloat16)


def _pairs(n, k):
    return [(i, i ^ k) for i in range(n)]


def _bits(n):
    bits = []
    k = 1
    while k < n:
        bits.append(k)
        k *= 2
    return bits


def tree_sum(x, axis):
    n = lax.axis_size(axis)
    for k in _bits(n):
        x = x + lax.ppermute(x, axis, _pairs(n, k))
    return x


def ring_sum(x, axis):
    n = lax.axis_size(axis)
    idx = lax.axis_index(axis)
    bits = _bits(n)
    for k in bits:
        half = x.shape[0] // 2
        upper = (idx // k) % 2 == 1
        lo, hi = x[:half], x[half:]
        keep = jnp.where(upper, hi, lo)
        send = jnp.where(upper, lo, hi)
        x = keep + lax.ppermute(send, axis, _pairs(n, k))
    for k in reversed(bits):
        upper = (idx // k) % 2 == 1
        other = lax.ppermute(x, axis, _pairs(n, k))
        x = jnp.where(upper, jnp.concatenate([other, x], 0), jnp.concatenate([x, other], 0))
    return x


def shards(queries, landmarks, targets, ridge):
    qhat = normalize(lax.all_gather(queries, "lm", axis=1, tiled=True))
    chat = normalize(landmarks)
    rows_dev = qhat.shape[0]
    lm_rows = chat.shape[0]
    width = qhat.shape[1]
    n_tg = targets.shape[1]
    block_rows = min(512, rows_dev)
    total_rows = float(rows_dev * lax.axis_size("dp"))
    first_dp = lax.axis_index("dp") == 0

    def tile_rows(block):
        scores = jnp.dot(block, chat.T, preferred_element_type=jnp.float32)
        tile = jnp.exp(2.0 * sharpness * scores).astype(jnp.bfloat16)
        values = tile.astype(jnp.float32)
        return (tile, jnp.sum(values * values, axis=0))

    tiles, column_sq = lax.map(tile_rows, qhat.reshape(rows_dev // block_rows, block_rows, width))
    kernel = tiles.reshape(rows_dev, lm_rows)
    rhs_part = lax.dot_general(
        kernel, targets, (((0,), (0,)), ((), ())), preferred_element_type=jnp.float32
    )
    stacked = ring_sum(jnp.concatenate([rhs_part, jnp.sum(column_sq, axis=0)[:, None]], 1), "dp")
    rhs = stacked[:, :n_tg] / total_rows
    precond = stacked[:, n_tg:] / total_rows + ridge[None, :]
    coefficients = jnp.zeros_like(rhs)
    residual = rhs
    direction = residual / precond
    norm_part = jnp.sum(residual * direction, axis=0)
    norm_now = None
    for step in range(ITERS):
        rounded = direction.astype(jnp.bfloat16)
        image_part = jnp.dot(kernel, rounded, preferred_element_type=jnp.float32)
        if norm_now is None:
            extra = jnp.zeros((rows_dev, 1), jnp.float32).at[:n_tg, 0].set(norm_part)
            summed = ring_sum(jnp.concatenate([image_part, extra], 1), "lm")
            query_image = summed[:, :n_tg]
            norm_now = summed[:n_tg, n_tg]
        else:
            query_image = ring_sum(image_part, "lm")
        back_part = lax.dot_general(
            kernel,
            query_image.astype(jnp.bfloat16),
            (((0,), (0,)), ((), ())),
            preferred_element_type=jnp.float32,
        )
        dot_part = jnp.sum(direction * back_part, axis=0) / total_rows + jnp.where(
            first_dp, ridge * jnp.sum(direction * direction, axis=0), 0.0
        )
        dot_all = tree_sum(tree_sum(dot_part, "dp"), "lm")
        back = ring_sum(back_part, "dp")
        image = back / total_rows + ridge[None, :] * direction
        alpha = norm_now / dot_all
        coefficients = coefficients + alpha[None, :] * direction
        residual = residual - alpha[None, :] * image
        if step + 1 < ITERS:
            scaled = residual / precond
            norm_next = tree_sum(jnp.sum(residual * scaled, axis=0), "lm")
            direction = scaled + (norm_next / norm_now)[None, :] * direction
            norm_now = norm_next
    rounded_coef = coefficients.astype(jnp.bfloat16)
    return ring_sum(jnp.dot(kernel, rounded_coef, preferred_element_type=jnp.float32), "lm")


def solution(mesh):
    return jax.shard_map(
        shards,
        mesh=mesh,
        in_specs=(P("dp", "lm"), P("lm", None), P("dp", None), P()),
        out_specs=P("dp", None),
        check_vma=False,
    )
```

```python
import jax
import jax.numpy as jnp
from jax import lax
from jax.sharding import PartitionSpec as P

ITERS = 2


sharpness = 8.0
epsilon = 1e-06


def normalize(rows):
    values = rows.astype(jnp.float32)
    scale = lax.rsqrt(jnp.sum(values * values, axis=1, keepdims=True) + epsilon)
    return (values * scale).astype(jnp.bfloat16)


def _pairs(n, k):
    return [(i, i ^ k) for i in range(n)]


def _bits(n):
    bits = []
    k = 1
    while k < n:
        bits.append(k)
        k *= 2
    return bits


def tree_sum(x, axis):
    n = lax.axis_size(axis)
    for k in _bits(n):
        x = x + lax.ppermute(x, axis, _pairs(n, k))
    return x


def ring_sum(x, axis, halvings=1):
    n = lax.axis_size(axis)
    idx = lax.axis_index(axis)
    bits = _bits(n)
    split, whole = bits[:halvings], bits[halvings:]
    for k in split:
        half = x.shape[0] // 2
        upper = (idx // k) % 2 == 1
        lo, hi = x[:half], x[half:]
        keep = jnp.where(upper, hi, lo)
        send = jnp.where(upper, lo, hi)
        x = keep + lax.ppermute(send, axis, _pairs(n, k))
    for k in whole:
        x = x + lax.ppermute(x, axis, _pairs(n, k))
    for k in reversed(split):
        upper = (idx // k) % 2 == 1
        other = lax.ppermute(x, axis, _pairs(n, k))
        x = jnp.where(upper, jnp.concatenate([other, x], 0), jnp.concatenate([x, other], 0))
    return x


def gather_rows(x, axis):
    n = lax.axis_size(axis)
    idx = lax.axis_index(axis)
    for k in _bits(n):
        upper = (idx // k) % 2 == 1
        other = lax.ppermute(x, axis, _pairs(n, k))
        x = jnp.where(upper, jnp.concatenate([other, x], 0), jnp.concatenate([x, other], 0))
    return x


def shards(queries, landmarks, targets, ridge):
    qhat = normalize(gather_rows(queries.T, "lm").T)
    chat = normalize(landmarks)
    rows_dev = qhat.shape[0]
    lm_rows = chat.shape[0]
    width = qhat.shape[1]
    n_tg = targets.shape[1]
    block_rows = min(512, rows_dev)
    total_rows = float(rows_dev * lax.axis_size("dp"))
    first_dp = lax.axis_index("dp") == 0

    def tile_rows(block):
        scores = jnp.dot(block, chat.T, preferred_element_type=jnp.float32)
        tile = jnp.exp(2.0 * sharpness * scores).astype(jnp.bfloat16)
        values = tile.astype(jnp.float32)
        return (tile, jnp.sum(values * values, axis=0))

    tiles, column_sq = lax.map(tile_rows, qhat.reshape(rows_dev // block_rows, block_rows, width))
    kernel = tiles.reshape(rows_dev, lm_rows)
    rhs_part = lax.dot_general(
        kernel, targets, (((0,), (0,)), ((), ())), preferred_element_type=jnp.float32
    )
    stacked = ring_sum(jnp.concatenate([rhs_part, jnp.sum(column_sq, axis=0)[:, None]], 1), "dp")
    rhs = stacked[:, :n_tg] / total_rows
    precond = stacked[:, n_tg:] / total_rows + ridge[None, :]
    coefficients = jnp.zeros_like(rhs)
    residual = rhs
    direction = residual / precond
    norm_part = jnp.sum(residual * direction, axis=0)
    norm_now = None
    for step in range(ITERS):
        rounded = direction.astype(jnp.bfloat16)
        image_part = jnp.dot(kernel, rounded, preferred_element_type=jnp.float32)
        if norm_now is None:
            extra = jnp.zeros((rows_dev, 1), jnp.float32).at[:n_tg, 0].set(norm_part)
            summed = ring_sum(jnp.concatenate([image_part, extra], 1), "lm")
            query_image = summed[:, :n_tg]
            norm_now = summed[:n_tg, n_tg]
        else:
            query_image = ring_sum(image_part, "lm")
        back_part = lax.dot_general(
            kernel,
            query_image.astype(jnp.bfloat16),
            (((0,), (0,)), ((), ())),
            preferred_element_type=jnp.float32,
        )
        dot_part = jnp.sum(direction * back_part, axis=0) / total_rows + jnp.where(
            first_dp, ridge * jnp.sum(direction * direction, axis=0), 0.0
        )
        dot_all = tree_sum(tree_sum(dot_part, "dp"), "lm")
        back = ring_sum(back_part, "dp")
        image = back / total_rows + ridge[None, :] * direction
        alpha = norm_now / dot_all
        coefficients = coefficients + alpha[None, :] * direction
        residual = residual - alpha[None, :] * image
        if step + 1 < ITERS:
            scaled = residual / precond
            norm_next = tree_sum(jnp.sum(residual * scaled, axis=0), "lm")
            direction = scaled + (norm_next / norm_now)[None, :] * direction
            norm_now = norm_next
    rounded_coef = coefficients.astype(jnp.bfloat16)
    return ring_sum(jnp.dot(kernel, rounded_coef, preferred_element_type=jnp.float32), "lm")


def solution(mesh):
    return jax.shard_map(
        shards,
        mesh=mesh,
        in_specs=(P("dp", "lm"), P("lm", None), P("dp", None), P()),
        out_specs=P("dp", None),
        check_vma=False,
    )
```

```python
import jax
import jax.numpy as jnp
from jax import lax
from jax.sharding import PartitionSpec as P

ITERS = 2


sharpness = 8.0
epsilon = 1e-06


def normalize(rows):
    values = rows.astype(jnp.float32)
    scale = lax.rsqrt(jnp.sum(values * values, axis=1, keepdims=True) + epsilon)
    return (values * scale).astype(jnp.bfloat16)


def _pairs(n, k):
    return [(i, i ^ k) for i in range(n)]


def _bits(n):
    bits = []
    k = 1
    while k < n:
        bits.append(k)
        k *= 2
    return bits


def tree_sum(x, axis):
    n = lax.axis_size(axis)
    for k in _bits(n):
        x = x + lax.ppermute(x, axis, _pairs(n, k))
    return x


def ring_sum(x, axis, halvings=1):
    n = lax.axis_size(axis)
    idx = lax.axis_index(axis)
    bits = _bits(n)
    split, whole = bits[:halvings], bits[halvings:]
    for k in split:
        half = x.shape[0] // 2
        upper = (idx // k) % 2 == 1
        lo, hi = x[:half], x[half:]
        keep = jnp.where(upper, hi, lo)
        send = jnp.where(upper, lo, hi)
        x = keep + lax.ppermute(send, axis, _pairs(n, k))
    for k in whole:
        x = x + lax.ppermute(x, axis, _pairs(n, k))
    for k in reversed(split):
        upper = (idx // k) % 2 == 1
        other = lax.ppermute(x, axis, _pairs(n, k))
        x = jnp.where(upper, jnp.concatenate([other, x], 0), jnp.concatenate([x, other], 0))
    return x


def gather_rows(x, axis):
    n = lax.axis_size(axis)
    idx = lax.axis_index(axis)
    for k in _bits(n):
        upper = (idx // k) % 2 == 1
        other = lax.ppermute(x, axis, _pairs(n, k))
        x = jnp.where(upper, jnp.concatenate([other, x], 0), jnp.concatenate([x, other], 0))
    return x


def shards(queries, landmarks, targets, ridge):
    qhat = normalize(gather_rows(queries.T, "lm").T)
    chat = normalize(landmarks)
    rows_dev = qhat.shape[0]
    lm_rows = chat.shape[0]
    width = qhat.shape[1]
    n_tg = targets.shape[1]
    block_rows = min(512, rows_dev)
    total_rows = float(rows_dev * lax.axis_size("dp"))
    first_dp = lax.axis_index("dp") == 0

    def tile_rows(carry, item):
        block, goal = item
        scores = jnp.dot(block, chat.T, preferred_element_type=jnp.float32)
        tile = jnp.exp(2.0 * sharpness * scores).astype(jnp.bfloat16)
        values = tile.astype(jnp.float32)
        rhs_acc, sq_acc = carry
        rhs_acc = rhs_acc + lax.dot_general(
            tile, goal, (((0,), (0,)), ((), ())), preferred_element_type=jnp.float32
        )
        return (rhs_acc, sq_acc + jnp.sum(values * values, axis=0)), tile

    n_blocks = rows_dev // block_rows
    start = (jnp.zeros((lm_rows, n_tg), jnp.float32), jnp.zeros((lm_rows,), jnp.float32))
    (rhs_part, sq_part), tiles = lax.scan(
        tile_rows,
        start,
        (qhat.reshape(n_blocks, block_rows, width), targets.reshape(n_blocks, block_rows, n_tg)),
    )
    kernel = tiles.reshape(rows_dev, lm_rows)
    stacked = ring_sum(jnp.concatenate([rhs_part, sq_part[:, None]], 1), "dp")
    rhs = stacked[:, :n_tg] / total_rows
    precond = stacked[:, n_tg:] / total_rows + ridge[None, :]
    coefficients = jnp.zeros_like(rhs)
    residual = rhs
    direction = residual / precond
    norm_part = jnp.sum(residual * direction, axis=0)
    norm_now = None
    for step in range(ITERS):
        rounded = lax.optimization_barrier(direction.astype(jnp.bfloat16))
        image_part = jnp.dot(kernel, rounded, preferred_element_type=jnp.float32)
        if norm_now is None:
            extra = jnp.zeros((rows_dev, 1), jnp.float32).at[:n_tg, 0].set(norm_part)
            summed = ring_sum(jnp.concatenate([image_part, extra], 1), "lm")
            query_image = summed[:, :n_tg]
            norm_now = summed[:n_tg, n_tg]
        else:
            query_image = ring_sum(image_part, "lm")
        back_part = lax.dot_general(
            kernel,
            lax.optimization_barrier(query_image.astype(jnp.bfloat16)),
            (((0,), (0,)), ((), ())),
            preferred_element_type=jnp.float32,
        )
        dot_part = jnp.sum(direction * back_part, axis=0) / total_rows + jnp.where(
            first_dp, ridge * jnp.sum(direction * direction, axis=0), 0.0
        )
        if step + 1 < ITERS:
            extra = jnp.zeros((lm_rows, 1), jnp.float32).at[:n_tg, 0].set(dot_part)
            summed = ring_sum(jnp.concatenate([back_part, extra], 1), "dp")
            back = summed[:, :n_tg]
            dot_all = tree_sum(summed[:n_tg, n_tg], "lm")
        else:
            back = ring_sum(back_part, "dp")
            dot_all = tree_sum(tree_sum(dot_part, "dp"), "lm")
        image = back / total_rows + ridge[None, :] * direction
        alpha = norm_now / dot_all
        coefficients = coefficients + alpha[None, :] * direction
        residual = residual - alpha[None, :] * image
        if step + 1 < ITERS:
            scaled = residual / precond
            norm_next = tree_sum(jnp.sum(residual * scaled, axis=0), "lm")
            direction = scaled + (norm_next / norm_now)[None, :] * direction
            norm_now = norm_next
    rounded_coef = lax.optimization_barrier(coefficients.astype(jnp.bfloat16))
    return ring_sum(jnp.dot(kernel, rounded_coef, preferred_element_type=jnp.float32), "lm")


def solution(mesh):
    return jax.shard_map(
        shards,
        mesh=mesh,
        in_specs=(P("dp", "lm"), P("lm", None), P("dp", None), P()),
        out_specs=P("dp", None),
        check_vma=False,
    )
```

```python
import jax
import jax.numpy as jnp
from jax import lax
from jax.sharding import PartitionSpec as P

ITERS = 2


sharpness = 8.0
epsilon = 1e-06


def normalize(rows):
    values = rows.astype(jnp.float32)
    scale = lax.rsqrt(jnp.sum(values * values, axis=1, keepdims=True) + epsilon)
    return (values * scale).astype(jnp.bfloat16)


RING_HIGH = {"dp": (8, 2), "lm": (16, 8)}


def _pairs(n, k, axis=None):
    size, high = RING_HIGH.get(axis, (0, 0))
    if n == size and k == high:
        lo = k // 2
        return [(i, i + (3 - 2 * ((i // lo) % 4)) * lo) for i in range(n)]
    return [(i, i ^ k) for i in range(n)]


def _order(n, axis):
    bits = _bits(n)
    size, high = RING_HIGH.get(axis, (0, 0))
    if n == size and axis == "dp":
        bits = [high] + [k for k in bits if k != high]
    return bits


def _bits(n):
    bits = []
    k = 1
    while k < n:
        bits.append(k)
        k *= 2
    return bits


def tree_sum(x, axis):
    n = lax.axis_size(axis)
    for k in _bits(n):
        x = x + lax.ppermute(x, axis, _pairs(n, k, axis))
    return x


def ring_sum(x, axis, halvings=1):
    n = lax.axis_size(axis)
    idx = lax.axis_index(axis)
    bits = _order(n, axis)
    split, whole = bits[:halvings], bits[halvings:]
    for k in split:
        half = x.shape[0] // 2
        upper = (idx // k) % 2 == 1
        lo, hi = x[:half], x[half:]
        keep = jnp.where(upper, hi, lo)
        send = jnp.where(upper, lo, hi)
        x = keep + lax.ppermute(send, axis, _pairs(n, k, axis))
    for k in whole:
        x = x + lax.ppermute(x, axis, _pairs(n, k, axis))
    for k in reversed(split):
        upper = (idx // k) % 2 == 1
        other = lax.ppermute(x, axis, _pairs(n, k, axis))
        x = jnp.where(upper, jnp.concatenate([other, x], 0), jnp.concatenate([x, other], 0))
    return x


def gather_rows(x, axis):
    n = lax.axis_size(axis)
    idx = lax.axis_index(axis)
    for k in _bits(n):
        upper = (idx // k) % 2 == 1
        other = lax.ppermute(x, axis, _pairs(n, k, axis))
        x = jnp.where(upper, jnp.concatenate([other, x], 0), jnp.concatenate([x, other], 0))
    return x


def shards(queries, landmarks, targets, ridge):
    qhat = normalize(gather_rows(queries.T, "lm").T)
    chat = normalize(landmarks)
    rows_dev = qhat.shape[0]
    lm_rows = chat.shape[0]
    width = qhat.shape[1]
    n_tg = targets.shape[1]
    block_rows = min(512, rows_dev)
    total_rows = float(rows_dev * lax.axis_size("dp"))
    first_dp = lax.axis_index("dp") == 0

    def tile_rows(block):
        scores = jnp.dot(block, chat.T, preferred_element_type=jnp.float32)
        tile = jnp.exp(2.0 * sharpness * scores).astype(jnp.bfloat16)
        values = tile.astype(jnp.float32)
        return (tile, jnp.sum(values * values, axis=0))

    tiles, column_sq = lax.map(tile_rows, qhat.reshape(rows_dev // block_rows, block_rows, width))
    kernel = tiles.reshape(rows_dev, lm_rows)
    rhs_part = lax.dot_general(
        kernel, targets, (((0,), (0,)), ((), ())), preferred_element_type=jnp.float32
    )
    sq_part = jnp.sum(column_sq, axis=0)
    stacked = ring_sum(jnp.concatenate([rhs_part, sq_part[:, None]], 1), "dp")
    rhs = stacked[:, :n_tg] / total_rows
    precond = stacked[:, n_tg:] / total_rows + ridge[None, :]
    coefficients = jnp.zeros_like(rhs)
    residual = rhs
    direction = residual / precond
    norm_part = jnp.sum(residual * direction, axis=0)
    norm_now = None
    for step in range(ITERS):
        rounded = lax.optimization_barrier(direction.astype(jnp.bfloat16))
        image_part = jnp.dot(kernel, rounded, preferred_element_type=jnp.float32)
        if norm_now is None:
            extra = jnp.zeros((rows_dev, 1), jnp.float32).at[:n_tg, 0].set(norm_part)
            summed = ring_sum(jnp.concatenate([image_part, extra], 1), "lm")
            query_image = summed[:, :n_tg]
            norm_now = summed[:n_tg, n_tg]
        else:
            query_image = ring_sum(image_part, "lm")
        back_part = lax.dot_general(
            kernel,
            lax.optimization_barrier(query_image.astype(jnp.bfloat16)),
            (((0,), (0,)), ((), ())),
            preferred_element_type=jnp.float32,
        )
        dot_part = jnp.sum(direction * back_part, axis=0) / total_rows + jnp.where(
            first_dp, ridge * jnp.sum(direction * direction, axis=0), 0.0
        )
        if step + 1 < ITERS:
            extra = jnp.zeros((lm_rows, 1), jnp.float32).at[:n_tg, 0].set(dot_part)
            summed = ring_sum(jnp.concatenate([back_part, extra], 1), "dp")
            back = summed[:, :n_tg]
            dot_all = tree_sum(summed[:n_tg, n_tg], "lm")
        else:
            back = ring_sum(back_part, "dp")
            dot_all = tree_sum(tree_sum(dot_part, "dp"), "lm")
        image = back / total_rows + ridge[None, :] * direction
        alpha = norm_now / dot_all
        coefficients = coefficients + alpha[None, :] * direction
        residual = residual - alpha[None, :] * image
        if step + 1 < ITERS:
            scaled = residual / precond
            norm_next = tree_sum(jnp.sum(residual * scaled, axis=0), "lm")
            direction = scaled + (norm_next / norm_now)[None, :] * direction
            norm_now = norm_next
    rounded_coef = lax.optimization_barrier(coefficients.astype(jnp.bfloat16))
    return ring_sum(jnp.dot(kernel, rounded_coef, preferred_element_type=jnp.float32), "lm")


def solution(mesh):
    return jax.shard_map(
        shards,
        mesh=mesh,
        in_specs=(P("dp", "lm"), P("lm", None), P("dp", None), P()),
        out_specs=P("dp", None),
        check_vma=False,
    )
```

```python
import jax
import jax.numpy as jnp
from jax import lax
from jax.sharding import PartitionSpec as P

ITERS = 2


sharpness = 8.0
epsilon = 1e-06


def normalize(rows):
    values = rows.astype(jnp.float32)
    scale = lax.rsqrt(jnp.sum(values * values, axis=1, keepdims=True) + epsilon)
    return (values * scale).astype(jnp.bfloat16)


RING_HIGH = {"dp": (8, 2), "lm": (16, 8)}


def _pairs(n, k, axis=None):
    size, high = RING_HIGH.get(axis, (0, 0))
    if n == size and k == high:
        lo = k // 2
        return [(i, i + (3 - 2 * ((i // lo) % 4)) * lo) for i in range(n)]
    return [(i, i ^ k) for i in range(n)]


def _order(n, axis):
    bits = _bits(n)
    size, high = RING_HIGH.get(axis, (0, 0))
    if n == size and axis == "dp":
        bits = [high] + [k for k in bits if k != high]
    return bits


def _bits(n):
    bits = []
    k = 1
    while k < n:
        bits.append(k)
        k *= 2
    return bits


def tree_sum(x, axis):
    n = lax.axis_size(axis)
    for k in _bits(n):
        x = x + lax.ppermute(x, axis, _pairs(n, k, axis))
    return x


def ring_sum(x, axis, halvings=1):
    n = lax.axis_size(axis)
    idx = lax.axis_index(axis)
    bits = _order(n, axis)
    split, whole = bits[:halvings], bits[halvings:]
    for k in split:
        half = x.shape[0] // 2
        upper = (idx // k) % 2 == 1
        lo, hi = x[:half], x[half:]
        keep = jnp.where(upper, hi, lo)
        send = jnp.where(upper, lo, hi)
        x = keep + lax.ppermute(send, axis, _pairs(n, k, axis))
    for k in whole:
        x = x + lax.ppermute(x, axis, _pairs(n, k, axis))
    for k in reversed(split):
        upper = (idx // k) % 2 == 1
        other = lax.ppermute(x, axis, _pairs(n, k, axis))
        x = jnp.where(upper, jnp.concatenate([other, x], 0), jnp.concatenate([x, other], 0))
    return x


def _dp_partner(d, k):
    if k == RING_HIGH["dp"][1]:
        lo = k // 2
        return d + (3 - 2 * ((d // lo) % 4)) * lo
    return d ^ k


def dp_sum(x):
    n_dp = lax.axis_size("dp")
    n_lm = lax.axis_size("lm")
    if n_dp != RING_HIGH["dp"][0] or n_lm % 2:
        return ring_sum(x, "dp")
    orders = ([2, 1, 4], [4, 2, 1])
    d = lax.axis_index("dp")
    second = lax.axis_index("lm") % 2 == 1

    def perm(step):
        return [
            (g, _dp_partner(g // n_lm, orders[(g % n_lm) % 2][step]) * n_lm + g % n_lm)
            for g in range(n_dp * n_lm)
        ]

    upper = jnp.where(second, (d // orders[1][0]) % 2 == 1, (d // orders[0][0]) % 2 == 1)
    half = x.shape[0] // 2
    lo, hi = x[:half], x[half:]
    keep = jnp.where(upper, hi, lo)
    send = jnp.where(upper, lo, hi)
    x = keep + lax.ppermute(send, ("dp", "lm"), perm(0))
    for step in range(1, len(orders[0])):
        x = x + lax.ppermute(x, ("dp", "lm"), perm(step))
    other = lax.ppermute(x, ("dp", "lm"), perm(0))
    return jnp.where(upper, jnp.concatenate([other, x], 0), jnp.concatenate([x, other], 0))


def gather_rows(x, axis):
    n = lax.axis_size(axis)
    idx = lax.axis_index(axis)
    for k in _bits(n):
        upper = (idx // k) % 2 == 1
        other = lax.ppermute(x, axis, _pairs(n, k, axis))
        x = jnp.where(upper, jnp.concatenate([other, x], 0), jnp.concatenate([x, other], 0))
    return x


def shards(queries, landmarks, targets, ridge):
    qhat = normalize(gather_rows(queries.T, "lm").T)
    chat = normalize(landmarks)
    rows_dev = qhat.shape[0]
    lm_rows = chat.shape[0]
    width = qhat.shape[1]
    n_tg = targets.shape[1]
    block_rows = min(512, rows_dev)
    total_rows = float(rows_dev * lax.axis_size("dp"))
    first_dp = lax.axis_index("dp") == 0

    def tile_rows(block):
        scores = jnp.dot(block, chat.T, preferred_element_type=jnp.float32)
        tile = jnp.exp(2.0 * sharpness * scores).astype(jnp.bfloat16)
        values = tile.astype(jnp.float32)
        return (tile, jnp.sum(values * values, axis=0))

    tiles, column_sq = lax.map(tile_rows, qhat.reshape(rows_dev // block_rows, block_rows, width))
    kernel = tiles.reshape(rows_dev, lm_rows)
    rhs_part = lax.dot_general(
        kernel, targets, (((0,), (0,)), ((), ())), preferred_element_type=jnp.float32
    )
    sq_part = jnp.sum(column_sq, axis=0)
    stacked = dp_sum(jnp.concatenate([rhs_part, sq_part[:, None]], 1))
    rhs = stacked[:, :n_tg] / total_rows
    precond = stacked[:, n_tg:] / total_rows + ridge[None, :]
    coefficients = jnp.zeros_like(rhs)
    residual = rhs
    direction = residual / precond
    norm_part = jnp.sum(residual * direction, axis=0)
    norm_now = None
    for step in range(ITERS):
        rounded = lax.optimization_barrier(direction.astype(jnp.bfloat16))
        image_part = jnp.dot(kernel, rounded, preferred_element_type=jnp.float32)
        if norm_now is None:
            extra = jnp.zeros((rows_dev, 1), jnp.float32).at[:n_tg, 0].set(norm_part)
            summed = ring_sum(jnp.concatenate([image_part, extra], 1), "lm")
            query_image = summed[:, :n_tg]
            norm_now = summed[:n_tg, n_tg]
        else:
            query_image = ring_sum(image_part, "lm")
        back_part = lax.dot_general(
            kernel,
            lax.optimization_barrier(query_image.astype(jnp.bfloat16)),
            (((0,), (0,)), ((), ())),
            preferred_element_type=jnp.float32,
        )
        dot_part = jnp.sum(direction * back_part, axis=0) / total_rows + jnp.where(
            first_dp, ridge * jnp.sum(direction * direction, axis=0), 0.0
        )
        if step + 1 < ITERS:
            extra = jnp.zeros((lm_rows, 1), jnp.float32).at[:n_tg, 0].set(dot_part)
            summed = dp_sum(jnp.concatenate([back_part, extra], 1))
            back = summed[:, :n_tg]
            dot_all = tree_sum(summed[:n_tg, n_tg], "lm")
        else:
            back = ring_sum(back_part, "dp")
            dot_all = tree_sum(tree_sum(dot_part, "dp"), "lm")
        image = back / total_rows + ridge[None, :] * direction
        alpha = norm_now / dot_all
        coefficients = coefficients + alpha[None, :] * direction
        residual = residual - alpha[None, :] * image
        if step + 1 < ITERS:
            scaled = residual / precond
            norm_next = tree_sum(jnp.sum(residual * scaled, axis=0), "lm")
            direction = scaled + (norm_next / norm_now)[None, :] * direction
            norm_now = norm_next
    rounded_coef = lax.optimization_barrier(coefficients.astype(jnp.bfloat16))
    return ring_sum(jnp.dot(kernel, rounded_coef, preferred_element_type=jnp.float32), "lm")


def solution(mesh):
    return jax.shard_map(
        shards,
        mesh=mesh,
        in_specs=(P("dp", "lm"), P("lm", None), P("dp", None), P()),
        out_specs=P("dp", None),
        check_vma=False,
    )
```

```python
import jax
import jax.numpy as jnp
from jax import lax
from jax.sharding import PartitionSpec as P

ITERS = 2


sharpness = 8.0
epsilon = 1e-06


def normalize(rows):
    values = rows.astype(jnp.float32)
    scale = lax.rsqrt(jnp.sum(values * values, axis=1, keepdims=True) + epsilon)
    return (values * scale).astype(jnp.bfloat16)


RING_HIGH = {"dp": (8, 2), "lm": (16, 8)}


def _pairs(n, k, axis=None):
    size, high = RING_HIGH.get(axis, (0, 0))
    if n == size and k == high:
        lo = k // 2
        return [(i, i + (3 - 2 * ((i // lo) % 4)) * lo) for i in range(n)]
    return [(i, i ^ k) for i in range(n)]


def _order(n, axis):
    bits = _bits(n)
    size, high = RING_HIGH.get(axis, (0, 0))
    if n == size and axis == "dp":
        bits = [high] + [k for k in bits if k != high]
    return bits


def _bits(n):
    bits = []
    k = 1
    while k < n:
        bits.append(k)
        k *= 2
    return bits


def tree_sum(x, axis):
    n = lax.axis_size(axis)
    for k in _bits(n):
        x = x + lax.ppermute(x, axis, _pairs(n, k, axis))
    return x


def ring_sum(x, axis, halvings=1):
    n = lax.axis_size(axis)
    idx = lax.axis_index(axis)
    bits = _order(n, axis)
    split, whole = bits[:halvings], bits[halvings:]
    for k in split:
        half = x.shape[0] // 2
        upper = (idx // k) % 2 == 1
        lo, hi = x[:half], x[half:]
        keep = jnp.where(upper, hi, lo)
        send = jnp.where(upper, lo, hi)
        x = keep + lax.ppermute(send, axis, _pairs(n, k, axis))
    if axis == "lm" and n == RING_HIGH["lm"][0] and split == [1]:
        second = whole[1:] + whole[:1]
        for step in range(len(whole)):
            mine = dict(_pairs(n, whole[step], axis))
            theirs = dict(_pairs(n, second[step], axis))
            perm = [(i, mine[i] if i % 2 == 0 else theirs[i]) for i in range(n)]
            x = x + lax.ppermute(x, axis, perm)
    else:
        for k in whole:
            x = x + lax.ppermute(x, axis, _pairs(n, k, axis))
    for k in reversed(split):
        upper = (idx // k) % 2 == 1
        other = lax.ppermute(x, axis, _pairs(n, k, axis))
        x = jnp.where(upper, jnp.concatenate([other, x], 0), jnp.concatenate([x, other], 0))
    return x


def _dp_partner(d, k):
    if k == RING_HIGH["dp"][1]:
        lo = k // 2
        return d + (3 - 2 * ((d // lo) % 4)) * lo
    return d ^ k


def dp_sum(x):
    n_dp = lax.axis_size("dp")
    n_lm = lax.axis_size("lm")
    if n_dp != RING_HIGH["dp"][0] or n_lm % 2:
        return ring_sum(x, "dp")
    orders = ([2, 1, 4], [4, 2, 1])
    d = lax.axis_index("dp")
    second = lax.axis_index("lm") % 2 == 1

    def perm(step):
        return [
            (g, _dp_partner(g // n_lm, orders[(g % n_lm) % 2][step]) * n_lm + g % n_lm)
            for g in range(n_dp * n_lm)
        ]

    upper = jnp.where(second, (d // orders[1][0]) % 2 == 1, (d // orders[0][0]) % 2 == 1)
    half = x.shape[0] // 2
    lo, hi = x[:half], x[half:]
    keep = jnp.where(upper, hi, lo)
    send = jnp.where(upper, lo, hi)
    x = keep + lax.ppermute(send, ("dp", "lm"), perm(0))
    for step in range(1, len(orders[0])):
        x = x + lax.ppermute(x, ("dp", "lm"), perm(step))
    other = lax.ppermute(x, ("dp", "lm"), perm(0))
    return jnp.where(upper, jnp.concatenate([other, x], 0), jnp.concatenate([x, other], 0))


def gather_rows(x, axis):
    n = lax.axis_size(axis)
    idx = lax.axis_index(axis)
    for k in _bits(n):
        upper = (idx // k) % 2 == 1
        other = lax.ppermute(x, axis, _pairs(n, k, axis))
        x = jnp.where(upper, jnp.concatenate([other, x], 0), jnp.concatenate([x, other], 0))
    return x


def shards(queries, landmarks, targets, ridge):
    qhat = normalize(gather_rows(queries.T, "lm").T)
    chat = normalize(landmarks)
    rows_dev = qhat.shape[0]
    lm_rows = chat.shape[0]
    width = qhat.shape[1]
    n_tg = targets.shape[1]
    block_rows = min(512, rows_dev)
    total_rows = float(rows_dev * lax.axis_size("dp"))
    first_dp = lax.axis_index("dp") == 0

    def tile_rows(block):
        scores = jnp.dot(block, chat.T, preferred_element_type=jnp.float32)
        tile = jnp.exp(2.0 * sharpness * scores).astype(jnp.bfloat16)
        values = tile.astype(jnp.float32)
        return (tile, jnp.sum(values * values, axis=0))

    tiles, column_sq = lax.map(tile_rows, qhat.reshape(rows_dev // block_rows, block_rows, width))
    kernel = tiles.reshape(rows_dev, lm_rows)
    rhs_part = lax.dot_general(
        kernel, targets, (((0,), (0,)), ((), ())), preferred_element_type=jnp.float32
    )
    sq_part = jnp.sum(column_sq, axis=0)
    stacked = dp_sum(jnp.concatenate([rhs_part, sq_part[:, None]], 1))
    rhs = stacked[:, :n_tg] / total_rows
    precond = stacked[:, n_tg:] / total_rows + ridge[None, :]
    coefficients = jnp.zeros_like(rhs)
    residual = rhs
    direction = residual / precond
    norm_part = jnp.sum(residual * direction, axis=0)
    norm_now = None
    for step in range(ITERS):
        rounded = lax.optimization_barrier(direction.astype(jnp.bfloat16))
        image_part = jnp.dot(kernel, rounded, preferred_element_type=jnp.float32)
        if norm_now is None:
            extra = jnp.zeros((rows_dev, 1), jnp.float32).at[:n_tg, 0].set(norm_part)
            summed = ring_sum(jnp.concatenate([image_part, extra], 1), "lm")
            query_image = summed[:, :n_tg]
            norm_now = summed[:n_tg, n_tg]
        else:
            query_image = ring_sum(image_part, "lm")
        back_part = lax.dot_general(
            kernel,
            lax.optimization_barrier(query_image.astype(jnp.bfloat16)),
            (((0,), (0,)), ((), ())),
            preferred_element_type=jnp.float32,
        )
        dot_part = jnp.sum(direction * back_part, axis=0) / total_rows + jnp.where(
            first_dp, ridge * jnp.sum(direction * direction, axis=0), 0.0
        )
        if step + 1 < ITERS:
            extra = jnp.zeros((lm_rows, 1), jnp.float32).at[:n_tg, 0].set(dot_part)
            summed = dp_sum(jnp.concatenate([back_part, extra], 1))
            back = summed[:, :n_tg]
            dot_all = tree_sum(summed[:n_tg, n_tg], "lm")
        else:
            back = ring_sum(back_part, "dp")
            dot_all = tree_sum(tree_sum(dot_part, "dp"), "lm")
        image = back / total_rows + ridge[None, :] * direction
        alpha = norm_now / dot_all
        coefficients = coefficients + alpha[None, :] * direction
        residual = residual - alpha[None, :] * image
        if step + 1 < ITERS:
            scaled = residual / precond
            norm_next = tree_sum(jnp.sum(residual * scaled, axis=0), "lm")
            direction = scaled + (norm_next / norm_now)[None, :] * direction
            norm_now = norm_next
    rounded_coef = lax.optimization_barrier(coefficients.astype(jnp.bfloat16))
    return ring_sum(jnp.dot(kernel, rounded_coef, preferred_element_type=jnp.float32), "lm")


def solution(mesh):
    return jax.shard_map(
        shards,
        mesh=mesh,
        in_specs=(P("dp", "lm"), P("lm", None), P("dp", None), P()),
        out_specs=P("dp", None),
        check_vma=False,
    )
```

```python
import jax
import jax.numpy as jnp
from jax import lax
from jax.sharding import PartitionSpec as P

ITERS = 2


sharpness = 8.0
epsilon = 1e-06


def normalize(rows):
    values = rows.astype(jnp.float32)
    scale = lax.rsqrt(jnp.sum(values * values, axis=1, keepdims=True) + epsilon)
    return (values * scale).astype(jnp.bfloat16)


RING_HIGH = {"dp": (8, 2), "lm": (16, 8)}


def _pairs(n, k, axis=None):
    size, high = RING_HIGH.get(axis, (0, 0))
    if n == size and k == high:
        lo = k // 2
        return [(i, i + (3 - 2 * ((i // lo) % 4)) * lo) for i in range(n)]
    return [(i, i ^ k) for i in range(n)]


def _order(n, axis):
    bits = _bits(n)
    size, high = RING_HIGH.get(axis, (0, 0))
    if n == size and axis == "dp":
        bits = [high] + [k for k in bits if k != high]
    return bits


def _bits(n):
    bits = []
    k = 1
    while k < n:
        bits.append(k)
        k *= 2
    return bits


def tree_sum(x, axis):
    n = lax.axis_size(axis)
    for k in _bits(n):
        x = x + lax.ppermute(x, axis, _pairs(n, k, axis))
    return x


def ring_sum(x, axis, halvings=1):
    n = lax.axis_size(axis)
    idx = lax.axis_index(axis)
    bits = _order(n, axis)
    split, whole = bits[:halvings], bits[halvings:]
    for k in split:
        half = x.shape[0] // 2
        upper = (idx // k) % 2 == 1
        lo, hi = x[:half], x[half:]
        keep = jnp.where(upper, hi, lo)
        send = jnp.where(upper, lo, hi)
        x = keep + lax.ppermute(send, axis, _pairs(n, k, axis))
    if axis == "lm" and n == RING_HIGH["lm"][0] and split == [1]:
        second = whole[1:] + whole[:1]
        for step in range(len(whole)):
            mine = dict(_pairs(n, whole[step], axis))
            theirs = dict(_pairs(n, second[step], axis))
            perm = [(i, mine[i] if i % 2 == 0 else theirs[i]) for i in range(n)]
            x = x + lax.ppermute(x, axis, perm)
    else:
        for k in whole:
            x = x + lax.ppermute(x, axis, _pairs(n, k, axis))
    for k in reversed(split):
        upper = (idx // k) % 2 == 1
        other = lax.ppermute(x, axis, _pairs(n, k, axis))
        x = jnp.where(upper, jnp.concatenate([other, x], 0), jnp.concatenate([x, other], 0))
    return x


def _dp_partner(d, k):
    if k == RING_HIGH["dp"][1]:
        lo = k // 2
        return d + (3 - 2 * ((d // lo) % 4)) * lo
    return d ^ k


def dp_sum(x):
    n_dp = lax.axis_size("dp")
    n_lm = lax.axis_size("lm")
    if n_dp != RING_HIGH["dp"][0] or n_lm % 2:
        return ring_sum(x, "dp")
    orders = ([2, 1, 4], [4, 2, 1])
    d = lax.axis_index("dp")
    second = lax.axis_index("lm") % 2 == 1

    def perm(step):
        return [
            (g, _dp_partner(g // n_lm, orders[(g % n_lm) % 2][step]) * n_lm + g % n_lm)
            for g in range(n_dp * n_lm)
        ]

    upper = jnp.where(second, (d // orders[1][0]) % 2 == 1, (d // orders[0][0]) % 2 == 1)
    half = x.shape[0] // 2
    lo, hi = x[:half], x[half:]
    keep = jnp.where(upper, hi, lo)
    send = jnp.where(upper, lo, hi)
    x = keep + lax.ppermute(send, ("dp", "lm"), perm(0))
    for step in range(1, len(orders[0])):
        x = x + lax.ppermute(x, ("dp", "lm"), perm(step))
    other = lax.ppermute(x, ("dp", "lm"), perm(0))
    return jnp.where(upper, jnp.concatenate([other, x], 0), jnp.concatenate([x, other], 0))


def gather_rows(x, axis):
    n = lax.axis_size(axis)
    idx = lax.axis_index(axis)
    for k in _bits(n):
        upper = (idx // k) % 2 == 1
        other = lax.ppermute(x, axis, _pairs(n, k, axis))
        x = jnp.where(upper, jnp.concatenate([other, x], 0), jnp.concatenate([x, other], 0))
    return x


def shards(queries, landmarks, targets, ridge):
    qhat = normalize(gather_rows(queries.T, "lm").T)
    chat = normalize(landmarks)
    rows_dev = qhat.shape[0]
    lm_rows = chat.shape[0]
    width = qhat.shape[1]
    n_tg = targets.shape[1]
    block_rows = min(512, rows_dev)
    total_rows = float(rows_dev * lax.axis_size("dp"))
    first_dp = lax.axis_index("dp") == 0

    def tile_rows(block):
        scores = jnp.dot(block, chat.T, preferred_element_type=jnp.float32)
        tile = jnp.exp(2.0 * sharpness * scores).astype(jnp.bfloat16)
        values = tile.astype(jnp.float32)
        return (tile, jnp.sum(values * values, axis=0))

    tiles, column_sq = lax.map(tile_rows, qhat.reshape(rows_dev // block_rows, block_rows, width))
    kernel = tiles.reshape(rows_dev, lm_rows)
    rhs_part, sq_part = lax.optimization_barrier((lax.dot_general(
        kernel, targets, (((0,), (0,)), ((), ())), preferred_element_type=jnp.float32
    ), jnp.sum(column_sq, axis=0)))
    stacked = dp_sum(jnp.concatenate([rhs_part, sq_part[:, None]], 1))
    rhs = stacked[:, :n_tg] / total_rows
    precond = stacked[:, n_tg:] / total_rows + ridge[None, :]
    coefficients = jnp.zeros_like(rhs)
    residual = rhs
    direction = residual / precond
    norm_part = jnp.sum(residual * direction, axis=0)
    norm_now = None
    for step in range(ITERS):
        rounded = lax.optimization_barrier(direction.astype(jnp.bfloat16))
        image_part = lax.optimization_barrier(jnp.dot(kernel, rounded, preferred_element_type=jnp.float32))
        if norm_now is None:
            extra = jnp.zeros((rows_dev, 1), jnp.float32).at[:n_tg, 0].set(norm_part)
            summed = ring_sum(jnp.concatenate([image_part, extra], 1), "lm")
            query_image = summed[:, :n_tg]
            norm_now = summed[:n_tg, n_tg]
        else:
            query_image = ring_sum(image_part, "lm")
        back_part = lax.optimization_barrier(lax.dot_general(
            kernel,
            lax.optimization_barrier(query_image.astype(jnp.bfloat16)),
            (((0,), (0,)), ((), ())),
            preferred_element_type=jnp.float32,
        ))
        dot_part = jnp.sum(direction * back_part, axis=0) / total_rows + jnp.where(
            first_dp, ridge * jnp.sum(direction * direction, axis=0), 0.0
        )
        if step + 1 < ITERS:
            extra = jnp.zeros((lm_rows, 1), jnp.float32).at[:n_tg, 0].set(dot_part)
            summed = dp_sum(jnp.concatenate([back_part, extra], 1))
            back = summed[:, :n_tg]
            dot_all = tree_sum(summed[:n_tg, n_tg], "lm")
        else:
            back = ring_sum(back_part, "dp")
            dot_all = tree_sum(tree_sum(dot_part, "dp"), "lm")
        image = back / total_rows + ridge[None, :] * direction
        alpha = norm_now / dot_all
        coefficients = coefficients + alpha[None, :] * direction
        residual = residual - alpha[None, :] * image
        if step + 1 < ITERS:
            scaled = residual / precond
            norm_next = tree_sum(jnp.sum(residual * scaled, axis=0), "lm")
            direction = scaled + (norm_next / norm_now)[None, :] * direction
            norm_now = norm_next
    rounded_coef = lax.optimization_barrier(coefficients.astype(jnp.bfloat16))
    return ring_sum(jnp.dot(kernel, rounded_coef, preferred_element_type=jnp.float32), "lm")


def solution(mesh):
    return jax.shard_map(
        shards,
        mesh=mesh,
        in_specs=(P("dp", "lm"), P("lm", None), P("dp", None), P()),
        out_specs=P("dp", None),
        check_vma=False,
    )
```

```python
import jax
import jax.numpy as jnp
from jax import lax
from jax.sharding import PartitionSpec as P

ITERS = 2


sharpness = 8.0
epsilon = 1e-06


def normalize(rows):
    values = rows.astype(jnp.float32)
    scale = lax.rsqrt(jnp.sum(values * values, axis=1, keepdims=True) + epsilon)
    return (values * scale).astype(jnp.bfloat16)


RING_HIGH = {"dp": (8, 2), "lm": (16, 8)}


def _pairs(n, k, axis=None):
    size, high = RING_HIGH.get(axis, (0, 0))
    if n == size and k == high:
        lo = k // 2
        return [(i, i + (3 - 2 * ((i // lo) % 4)) * lo) for i in range(n)]
    return [(i, i ^ k) for i in range(n)]


def _order(n, axis):
    bits = _bits(n)
    size, high = RING_HIGH.get(axis, (0, 0))
    if n == size and axis == "dp":
        bits = [high] + [k for k in bits if k != high]
    return bits


def _bits(n):
    bits = []
    k = 1
    while k < n:
        bits.append(k)
        k *= 2
    return bits


def tree_sum(x, axis):
    n = lax.axis_size(axis)
    for k in _bits(n):
        x = x + lax.ppermute(x, axis, _pairs(n, k, axis))
    return x


def ring_sum(x, axis, halvings=1, tiny=None):
    n = lax.axis_size(axis)
    idx = lax.axis_index(axis)
    bits = _order(n, axis)
    split, whole = bits[:halvings], bits[halvings:]

    def add(x, tiny, perm):
        if tiny is None:
            return x + lax.ppermute(x, axis, perm), None
        got, got_tiny = lax.ppermute((x, tiny), axis, perm)
        return x + got, tiny + got_tiny

    for k in split:
        half = x.shape[0] // 2
        upper = (idx // k) % 2 == 1
        lo, hi = x[:half], x[half:]
        keep = jnp.where(upper, hi, lo)
        send = jnp.where(upper, lo, hi)
        if tiny is None:
            x = keep + lax.ppermute(send, axis, _pairs(n, k, axis))
        else:
            got, got_tiny = lax.ppermute((send, tiny), axis, _pairs(n, k, axis))
            x, tiny = keep + got, tiny + got_tiny
    if axis == "lm" and n == RING_HIGH["lm"][0] and split == [1]:
        second = whole[1:] + whole[:1]
        for step in range(len(whole)):
            mine = dict(_pairs(n, whole[step], axis))
            theirs = dict(_pairs(n, second[step], axis))
            x, tiny = add(x, tiny, [(i, mine[i] if i % 2 == 0 else theirs[i]) for i in range(n)])
    else:
        for k in whole:
            x, tiny = add(x, tiny, _pairs(n, k, axis))
    for k in reversed(split):
        upper = (idx // k) % 2 == 1
        other = lax.ppermute(x, axis, _pairs(n, k, axis))
        x = jnp.where(upper, jnp.concatenate([other, x], 0), jnp.concatenate([x, other], 0))
    if tiny is None:
        return x
    return x, tiny


def _dp_partner(d, k):
    if k == RING_HIGH["dp"][1]:
        lo = k // 2
        return d + (3 - 2 * ((d // lo) % 4)) * lo
    return d ^ k


def dp_sum(x):
    n_dp = lax.axis_size("dp")
    n_lm = lax.axis_size("lm")
    if n_dp != RING_HIGH["dp"][0] or n_lm % 2:
        return ring_sum(x, "dp")
    orders = ([2, 1, 4], [4, 2, 1])
    d = lax.axis_index("dp")
    second = lax.axis_index("lm") % 2 == 1

    def perm(step):
        return [
            (g, _dp_partner(g // n_lm, orders[(g % n_lm) % 2][step]) * n_lm + g % n_lm)
            for g in range(n_dp * n_lm)
        ]

    upper = jnp.where(second, (d // orders[1][0]) % 2 == 1, (d // orders[0][0]) % 2 == 1)
    half = x.shape[0] // 2
    lo, hi = x[:half], x[half:]
    keep = jnp.where(upper, hi, lo)
    send = jnp.where(upper, lo, hi)
    x = keep + lax.ppermute(send, ("dp", "lm"), perm(0))
    for step in range(1, len(orders[0])):
        x = x + lax.ppermute(x, ("dp", "lm"), perm(step))
    other = lax.ppermute(x, ("dp", "lm"), perm(0))
    return jnp.where(upper, jnp.concatenate([other, x], 0), jnp.concatenate([x, other], 0))


def gather_rows(x, axis):
    n = lax.axis_size(axis)
    idx = lax.axis_index(axis)
    for k in _bits(n):
        upper = (idx // k) % 2 == 1
        other = lax.ppermute(x, axis, _pairs(n, k, axis))
        x = jnp.where(upper, jnp.concatenate([other, x], 0), jnp.concatenate([x, other], 0))
    return x


def shards(queries, landmarks, targets, ridge):
    qhat = normalize(gather_rows(queries.T, "lm").T)
    chat = normalize(landmarks)
    rows_dev = qhat.shape[0]
    lm_rows = chat.shape[0]
    width = qhat.shape[1]
    n_tg = targets.shape[1]
    block_rows = min(512, rows_dev)
    total_rows = float(rows_dev * lax.axis_size("dp"))
    first_dp = lax.axis_index("dp") == 0

    def tile_rows(block):
        scores = jnp.dot(block, chat.T, preferred_element_type=jnp.float32)
        tile = jnp.exp(2.0 * sharpness * scores).astype(jnp.bfloat16)
        values = tile.astype(jnp.float32)
        return (tile, jnp.sum(values * values, axis=0))

    tiles, column_sq = lax.map(tile_rows, qhat.reshape(rows_dev // block_rows, block_rows, width))
    kernel = tiles.reshape(rows_dev, lm_rows)
    rhs_part, sq_part = lax.optimization_barrier((lax.dot_general(
        kernel, targets, (((0,), (0,)), ((), ())), preferred_element_type=jnp.float32
    ), jnp.sum(column_sq, axis=0)))
    stacked = dp_sum(jnp.concatenate([rhs_part, sq_part[:, None]], 1))
    rhs = stacked[:, :n_tg] / total_rows
    precond = stacked[:, n_tg:] / total_rows + ridge[None, :]
    coefficients = jnp.zeros_like(rhs)
    residual = rhs
    direction = residual / precond
    norm_part = jnp.sum(residual * direction, axis=0)
    norm_now = None
    for step in range(ITERS):
        rounded = lax.optimization_barrier(direction.astype(jnp.bfloat16))
        image_part = lax.optimization_barrier(jnp.dot(kernel, rounded, preferred_element_type=jnp.float32))
        if norm_now is None:
            query_image, norm_now = ring_sum(image_part.astype(jnp.bfloat16), "lm", tiny=norm_part)
        else:
            query_image = ring_sum(image_part.astype(jnp.bfloat16), "lm")
        back_part = lax.optimization_barrier(lax.dot_general(
            kernel,
            lax.optimization_barrier(query_image.astype(jnp.bfloat16)),
            (((0,), (0,)), ((), ())),
            preferred_element_type=jnp.float32,
        ))
        dot_part = jnp.sum(direction * back_part, axis=0) / total_rows + jnp.where(
            first_dp, ridge * jnp.sum(direction * direction, axis=0), 0.0
        )
        if step + 1 < ITERS:
            extra = jnp.zeros((lm_rows, 1), jnp.float32).at[:n_tg, 0].set(dot_part)
            summed = dp_sum(jnp.concatenate([back_part, extra], 1))
            back = summed[:, :n_tg]
            dot_all = tree_sum(summed[:n_tg, n_tg], "lm")
        else:
            back = ring_sum(back_part, "dp")
            dot_all = tree_sum(tree_sum(dot_part, "dp"), "lm")
        image = back / total_rows + ridge[None, :] * direction
        alpha = norm_now / dot_all
        coefficients = coefficients + alpha[None, :] * direction
        residual = residual - alpha[None, :] * image
        if step + 1 < ITERS:
            scaled = residual / precond
            norm_next = tree_sum(jnp.sum(residual * scaled, axis=0), "lm")
            direction = scaled + (norm_next / norm_now)[None, :] * direction
            norm_now = norm_next
    rounded_coef = lax.optimization_barrier(coefficients.astype(jnp.bfloat16))
    return ring_sum(jnp.dot(kernel, rounded_coef, preferred_element_type=jnp.float32), "lm")


def solution(mesh):
    return jax.shard_map(
        shards,
        mesh=mesh,
        in_specs=(P("dp", "lm"), P("lm", None), P("dp", None), P()),
        out_specs=P("dp", None),
        check_vma=False,
    )
```

```python
import jax
import jax.numpy as jnp
from jax import lax
from jax.sharding import PartitionSpec as P

ITERS = 2


sharpness = 8.0
epsilon = 1e-06


def normalize(rows):
    values = rows.astype(jnp.float32)
    scale = lax.rsqrt(jnp.sum(values * values, axis=1, keepdims=True) + epsilon)
    return (values * scale).astype(jnp.bfloat16)


RING_HIGH = {"dp": (8, 2), "lm": (16, 8)}


def _pairs(n, k, axis=None):
    size, high = RING_HIGH.get(axis, (0, 0))
    if n == size and k == high:
        lo = k // 2
        return [(i, i + (3 - 2 * ((i // lo) % 4)) * lo) for i in range(n)]
    return [(i, i ^ k) for i in range(n)]


def _order(n, axis):
    bits = _bits(n)
    size, high = RING_HIGH.get(axis, (0, 0))
    if n == size and axis == "dp":
        bits = [high] + [k for k in bits if k != high]
    return bits


def _bits(n):
    bits = []
    k = 1
    while k < n:
        bits.append(k)
        k *= 2
    return bits


def tree_sum(x, axis):
    n = lax.axis_size(axis)
    for k in _bits(n):
        x = x + lax.ppermute(x, axis, _pairs(n, k, axis))
    return x


def ring_sum(x, axis, halvings=1, tiny=None):
    n = lax.axis_size(axis)
    idx = lax.axis_index(axis)
    bits = _order(n, axis)
    split, whole = bits[:halvings], bits[halvings:]

    def add(x, tiny, perm):
        if tiny is None:
            return x + lax.ppermute(x, axis, perm), None
        got, got_tiny = lax.ppermute((x, tiny), axis, perm)
        return x + got, tiny + got_tiny

    for k in split:
        half = x.shape[0] // 2
        upper = (idx // k) % 2 == 1
        lo, hi = x[:half], x[half:]
        keep = jnp.where(upper, hi, lo)
        send = jnp.where(upper, lo, hi)
        if tiny is None:
            x = keep + lax.ppermute(send, axis, _pairs(n, k, axis))
        else:
            got, got_tiny = lax.ppermute((send, tiny), axis, _pairs(n, k, axis))
            x, tiny = keep + got, tiny + got_tiny
    if axis == "lm" and n == RING_HIGH["lm"][0] and split == [1]:
        second = whole[1:] + whole[:1]
        for step in range(len(whole)):
            mine = dict(_pairs(n, whole[step], axis))
            theirs = dict(_pairs(n, second[step], axis))
            x, tiny = add(x, tiny, [(i, mine[i] if i % 2 == 0 else theirs[i]) for i in range(n)])
    else:
        for k in whole:
            x, tiny = add(x, tiny, _pairs(n, k, axis))
    for k in reversed(split):
        upper = (idx // k) % 2 == 1
        other = lax.ppermute(x, axis, _pairs(n, k, axis))
        x = jnp.where(upper, jnp.concatenate([other, x], 0), jnp.concatenate([x, other], 0))
    if tiny is None:
        return x
    return x, tiny


def _dp_partner(d, k):
    if k == RING_HIGH["dp"][1]:
        lo = k // 2
        return d + (3 - 2 * ((d // lo) % 4)) * lo
    return d ^ k


def dp_sum(x):
    n_dp = lax.axis_size("dp")
    n_lm = lax.axis_size("lm")
    if n_dp != RING_HIGH["dp"][0] or n_lm % 2:
        return ring_sum(x, "dp")
    orders = ([2, 1, 4], [4, 2, 1])
    d = lax.axis_index("dp")
    second = lax.axis_index("lm") % 2 == 1

    def perm(step):
        return [
            (g, _dp_partner(g // n_lm, orders[(g % n_lm) % 2][step]) * n_lm + g % n_lm)
            for g in range(n_dp * n_lm)
        ]

    upper = jnp.where(second, (d // orders[1][0]) % 2 == 1, (d // orders[0][0]) % 2 == 1)
    half = x.shape[0] // 2
    lo, hi = x[:half], x[half:]
    keep = jnp.where(upper, hi, lo)
    send = jnp.where(upper, lo, hi)
    x = keep + lax.ppermute(send, ("dp", "lm"), perm(0))
    for step in range(1, len(orders[0])):
        x = x + lax.ppermute(x, ("dp", "lm"), perm(step))
    other = lax.ppermute(x, ("dp", "lm"), perm(0))
    return jnp.where(upper, jnp.concatenate([other, x], 0), jnp.concatenate([x, other], 0))


def gather_rows(x, axis):
    n = lax.axis_size(axis)
    idx = lax.axis_index(axis)
    bits = _bits(n)
    if not (axis == "lm" and n == RING_HIGH["lm"][0]):
        for k in bits:
            upper = (idx // k) % 2 == 1
            other = lax.ppermute(x, axis, _pairs(n, k, axis))
            x = jnp.where(upper, jnp.concatenate([other, x], 0), jnp.concatenate([x, other], 0))
        return x
    first = bits
    second = bits[:1] + bits[2:] + bits[1:2]
    block = x.shape[0]
    on_second = idx % 2 == 1
    for step in range(len(bits)):
        mine = dict(_pairs(n, first[step], axis))
        theirs = dict(_pairs(n, second[step], axis))
        perm = [(i, mine[i] if i % 2 == 0 else theirs[i]) for i in range(n)]
        upper = jnp.where(on_second, (idx // second[step]) % 2 == 1, (idx // first[step]) % 2 == 1)
        other = lax.ppermute(x, axis, perm)
        x = jnp.where(upper, jnp.concatenate([other, x], 0), jnp.concatenate([x, other], 0))

    def place(i):
        return sum(((i // k) % 2) << p for p, k in enumerate(second))

    ordered = jnp.concatenate([x[place(i) * block:(place(i) + 1) * block] for i in range(n)], 0)
    return jnp.where(on_second, ordered, x)


def shards(queries, landmarks, targets, ridge):
    qhat = normalize(gather_rows(queries.T, "lm").T)
    chat = normalize(landmarks)
    rows_dev = qhat.shape[0]
    lm_rows = chat.shape[0]
    width = qhat.shape[1]
    n_tg = targets.shape[1]
    block_rows = min(512, rows_dev)
    total_rows = float(rows_dev * lax.axis_size("dp"))
    first_dp = lax.axis_index("dp") == 0

    def tile_rows(block):
        scores = jnp.dot(block, chat.T, preferred_element_type=jnp.float32)
        tile = jnp.exp(2.0 * sharpness * scores).astype(jnp.bfloat16)
        values = tile.astype(jnp.float32)
        return (tile, jnp.sum(values * values, axis=0))

    tiles, column_sq = lax.map(tile_rows, qhat.reshape(rows_dev // block_rows, block_rows, width))
    kernel = tiles.reshape(rows_dev, lm_rows)
    rhs_part, sq_part = lax.optimization_barrier((lax.dot_general(
        kernel, targets, (((0,), (0,)), ((), ())), preferred_element_type=jnp.float32
    ), jnp.sum(column_sq, axis=0)))
    stacked = dp_sum(jnp.concatenate([rhs_part, sq_part[:, None]], 1))
    rhs = stacked[:, :n_tg] / total_rows
    precond = stacked[:, n_tg:] / total_rows + ridge[None, :]
    coefficients = jnp.zeros_like(rhs)
    residual = rhs
    direction = residual / precond
    norm_part = jnp.sum(residual * direction, axis=0)
    norm_now = None
    for step in range(ITERS):
        rounded = lax.optimization_barrier(direction.astype(jnp.bfloat16))
        image_part = lax.optimization_barrier(jnp.dot(kernel, rounded, preferred_element_type=jnp.float32))
        if norm_now is None:
            query_image, norm_now = ring_sum(image_part.astype(jnp.bfloat16), "lm", tiny=norm_part)
        else:
            query_image = ring_sum(image_part.astype(jnp.bfloat16), "lm")
        back_part = lax.optimization_barrier(lax.dot_general(
            kernel,
            lax.optimization_barrier(query_image.astype(jnp.bfloat16)),
            (((0,), (0,)), ((), ())),
            preferred_element_type=jnp.float32,
        ))
        dot_part = jnp.sum(direction * back_part, axis=0) / total_rows + jnp.where(
            first_dp, ridge * jnp.sum(direction * direction, axis=0), 0.0
        )
        if step + 1 < ITERS:
            extra = jnp.zeros((lm_rows, 1), jnp.float32).at[:n_tg, 0].set(dot_part)
            summed = dp_sum(jnp.concatenate([back_part, extra], 1))
            back = summed[:, :n_tg]
            dot_all = tree_sum(summed[:n_tg, n_tg], "lm")
        else:
            back = ring_sum(back_part, "dp")
            dot_all = tree_sum(tree_sum(dot_part, "dp"), "lm")
        image = back / total_rows + ridge[None, :] * direction
        alpha = norm_now / dot_all
        coefficients = coefficients + alpha[None, :] * direction
        residual = residual - alpha[None, :] * image
        if step + 1 < ITERS:
            scaled = residual / precond
            norm_next = tree_sum(jnp.sum(residual * scaled, axis=0), "lm")
            direction = scaled + (norm_next / norm_now)[None, :] * direction
            norm_now = norm_next
    rounded_coef = lax.optimization_barrier(coefficients.astype(jnp.bfloat16))
    return ring_sum(jnp.dot(kernel, rounded_coef, preferred_element_type=jnp.float32), "lm")


def solution(mesh):
    return jax.shard_map(
        shards,
        mesh=mesh,
        in_specs=(P("dp", "lm"), P("lm", None), P("dp", None), P()),
        out_specs=P("dp", None),
        check_vma=False,
    )
```

```python
import jax
import jax.numpy as jnp
from jax import lax
from jax.sharding import PartitionSpec as P

ITERS = 2


sharpness = 8.0
epsilon = 1e-06


def normalize(rows):
    values = rows.astype(jnp.float32)
    scale = lax.rsqrt(jnp.sum(values * values, axis=1, keepdims=True) + epsilon)
    return (values * scale).astype(jnp.bfloat16)


RING_HIGH = {"dp": (8, 2), "lm": (16, 8)}


def _pairs(n, k, axis=None):
    size, high = RING_HIGH.get(axis, (0, 0))
    if n == size and k == high:
        lo = k // 2
        return [(i, i + (3 - 2 * ((i // lo) % 4)) * lo) for i in range(n)]
    return [(i, i ^ k) for i in range(n)]


def _order(n, axis):
    bits = _bits(n)
    size, high = RING_HIGH.get(axis, (0, 0))
    if n == size and axis == "dp":
        bits = [high] + [k for k in bits if k != high]
    return bits


def _bits(n):
    bits = []
    k = 1
    while k < n:
        bits.append(k)
        k *= 2
    return bits


def tree_sum(x, axis):
    n = lax.axis_size(axis)
    for k in _bits(n):
        x = x + lax.ppermute(x, axis, _pairs(n, k, axis))
    return x


def ring_sum(x, axis, halvings=1, tiny=None):
    n = lax.axis_size(axis)
    idx = lax.axis_index(axis)
    bits = _order(n, axis)
    split, whole = bits[:halvings], bits[halvings:]

    def add(x, tiny, perm):
        if tiny is None:
            return x + lax.ppermute(x, axis, perm), None
        got, got_tiny = lax.ppermute((x, tiny), axis, perm)
        return x + got, tiny + got_tiny

    for k in split:
        half = x.shape[0] // 2
        upper = (idx // k) % 2 == 1
        lo, hi = x[:half], x[half:]
        keep = jnp.where(upper, hi, lo)
        send = jnp.where(upper, lo, hi)
        if tiny is None:
            x = keep + lax.ppermute(send, axis, _pairs(n, k, axis))
        else:
            got, got_tiny = lax.ppermute((send, tiny), axis, _pairs(n, k, axis))
            x, tiny = keep + got, tiny + got_tiny
    if axis == "lm" and n == RING_HIGH["lm"][0] and split == [1]:
        second = whole[1:] + whole[:1]
        for step in range(len(whole)):
            mine = dict(_pairs(n, whole[step], axis))
            theirs = dict(_pairs(n, second[step], axis))
            x, tiny = add(x, tiny, [(i, mine[i] if i % 2 == 0 else theirs[i]) for i in range(n)])
    else:
        for k in whole:
            x, tiny = add(x, tiny, _pairs(n, k, axis))
    for k in reversed(split):
        upper = (idx // k) % 2 == 1
        other = lax.ppermute(x, axis, _pairs(n, k, axis))
        x = jnp.where(upper, jnp.concatenate([other, x], 0), jnp.concatenate([x, other], 0))
    if tiny is None:
        return x
    return x, tiny


def _dp_partner(d, k):
    if k == RING_HIGH["dp"][1]:
        lo = k // 2
        return d + (3 - 2 * ((d // lo) % 4)) * lo
    return d ^ k


def dp_sum(x):
    n_dp = lax.axis_size("dp")
    n_lm = lax.axis_size("lm")
    if n_dp != RING_HIGH["dp"][0] or n_lm % 2:
        return ring_sum(x, "dp")
    orders = ([2, 1, 4], [4, 2, 1])
    d = lax.axis_index("dp")
    second = lax.axis_index("lm") % 2 == 1

    def perm(step):
        return [
            (g, _dp_partner(g // n_lm, orders[(g % n_lm) % 2][step]) * n_lm + g % n_lm)
            for g in range(n_dp * n_lm)
        ]

    upper = jnp.where(second, (d // orders[1][0]) % 2 == 1, (d // orders[0][0]) % 2 == 1)
    half = x.shape[0] // 2
    lo, hi = x[:half], x[half:]
    keep = jnp.where(upper, hi, lo)
    send = jnp.where(upper, lo, hi)
    x = keep + _moved(send, perm(0))
    for step in range(1, len(orders[0])):
        x = x + _moved(x, perm(step))
    other = _moved(x, perm(0))
    return jnp.where(upper, jnp.concatenate([other, x], 0), jnp.concatenate([x, other], 0))


def _moved(x, perm):
    half = x.shape[0] // 2
    return jnp.concatenate(
        [lax.ppermute(x[:half], ("dp", "lm"), perm), lax.ppermute(x[half:], ("dp", "lm"), perm)], 0
    )


def gather_rows(x, axis):
    n = lax.axis_size(axis)
    idx = lax.axis_index(axis)
    bits = _bits(n)
    if not (axis == "lm" and n == RING_HIGH["lm"][0]):
        for k in bits:
            upper = (idx // k) % 2 == 1
            other = lax.ppermute(x, axis, _pairs(n, k, axis))
            x = jnp.where(upper, jnp.concatenate([other, x], 0), jnp.concatenate([x, other], 0))
        return x
    first = bits
    second = bits[:1] + bits[2:] + bits[1:2]
    block = x.shape[0]
    on_second = idx % 2 == 1
    for step in range(len(bits)):
        mine = dict(_pairs(n, first[step], axis))
        theirs = dict(_pairs(n, second[step], axis))
        perm = [(i, mine[i] if i % 2 == 0 else theirs[i]) for i in range(n)]
        upper = jnp.where(on_second, (idx // second[step]) % 2 == 1, (idx // first[step]) % 2 == 1)
        other = lax.ppermute(x, axis, perm)
        x = jnp.where(upper, jnp.concatenate([other, x], 0), jnp.concatenate([x, other], 0))

    def place(i):
        return sum(((i // k) % 2) << p for p, k in enumerate(second))

    ordered = jnp.concatenate([x[place(i) * block:(place(i) + 1) * block] for i in range(n)], 0)
    return jnp.where(on_second, ordered, x)


def shards(queries, landmarks, targets, ridge):
    qhat = normalize(gather_rows(queries.T, "lm").T)
    chat = normalize(landmarks)
    rows_dev = qhat.shape[0]
    lm_rows = chat.shape[0]
    width = qhat.shape[1]
    n_tg = targets.shape[1]
    block_rows = min(512, rows_dev)
    total_rows = float(rows_dev * lax.axis_size("dp"))
    first_dp = lax.axis_index("dp") == 0

    def tile_rows(block):
        scores = jnp.dot(block, chat.T, preferred_element_type=jnp.float32)
        tile = jnp.exp(2.0 * sharpness * scores).astype(jnp.bfloat16)
        values = tile.astype(jnp.float32)
        return (tile, jnp.sum(values * values, axis=0))

    tiles, column_sq = lax.map(tile_rows, qhat.reshape(rows_dev // block_rows, block_rows, width))
    kernel = tiles.reshape(rows_dev, lm_rows)
    rhs_part, sq_part = lax.optimization_barrier((lax.dot_general(
        kernel, targets, (((0,), (0,)), ((), ())), preferred_element_type=jnp.float32
    ), jnp.sum(column_sq, axis=0)))
    stacked = dp_sum(jnp.concatenate([rhs_part, sq_part[:, None]], 1))
    rhs = stacked[:, :n_tg] / total_rows
    precond = stacked[:, n_tg:] / total_rows + ridge[None, :]
    coefficients = jnp.zeros_like(rhs)
    residual = rhs
    direction = residual / precond
    norm_part = jnp.sum(residual * direction, axis=0)
    norm_now = None
    for step in range(ITERS):
        rounded = lax.optimization_barrier(direction.astype(jnp.bfloat16))
        image_part = lax.optimization_barrier(jnp.dot(kernel, rounded, preferred_element_type=jnp.float32))
        if norm_now is None:
            query_image, norm_now = ring_sum(image_part.astype(jnp.bfloat16), "lm", tiny=norm_part)
        else:
            query_image = ring_sum(image_part.astype(jnp.bfloat16), "lm")
        back_part = lax.optimization_barrier(lax.dot_general(
            kernel,
            lax.optimization_barrier(query_image.astype(jnp.bfloat16)),
            (((0,), (0,)), ((), ())),
            preferred_element_type=jnp.float32,
        ))
        dot_part = jnp.sum(direction * back_part, axis=0) / total_rows + jnp.where(
            first_dp, ridge * jnp.sum(direction * direction, axis=0), 0.0
        )
        if step + 1 < ITERS:
            extra = jnp.zeros((lm_rows, 1), jnp.float32).at[:n_tg, 0].set(dot_part)
            summed = dp_sum(jnp.concatenate([back_part, extra], 1))
            back = summed[:, :n_tg]
            dot_all = tree_sum(summed[:n_tg, n_tg], "lm")
        else:
            back = ring_sum(back_part, "dp")
            dot_all = tree_sum(tree_sum(dot_part, "dp"), "lm")
        image = back / total_rows + ridge[None, :] * direction
        alpha = norm_now / dot_all
        coefficients = coefficients + alpha[None, :] * direction
        residual = residual - alpha[None, :] * image
        if step + 1 < ITERS:
            scaled = residual / precond
            norm_next = tree_sum(jnp.sum(residual * scaled, axis=0), "lm")
            direction = scaled + (norm_next / norm_now)[None, :] * direction
            norm_now = norm_next
    rounded_coef = lax.optimization_barrier(coefficients.astype(jnp.bfloat16))
    return ring_sum(jnp.dot(kernel, rounded_coef, preferred_element_type=jnp.float32), "lm")


def solution(mesh):
    return jax.shard_map(
        shards,
        mesh=mesh,
        in_specs=(P("dp", "lm"), P("lm", None), P("dp", None), P()),
        out_specs=P("dp", None),
        check_vma=False,
    )
```

```python
import jax
import jax.numpy as jnp
from jax import lax
from jax.sharding import PartitionSpec as P

ITERS = 2


sharpness = 8.0
epsilon = 1e-06


def normalize(rows):
    values = rows.astype(jnp.float32)
    scale = lax.rsqrt(jnp.sum(values * values, axis=1, keepdims=True) + epsilon)
    return (values * scale).astype(jnp.bfloat16)


RING_HIGH = {"dp": (8, 2), "lm": (16, 8)}


def _pairs(n, k, axis=None):
    size, high = RING_HIGH.get(axis, (0, 0))
    if n == size and k == high:
        lo = k // 2
        return [(i, i + (3 - 2 * ((i // lo) % 4)) * lo) for i in range(n)]
    return [(i, i ^ k) for i in range(n)]


def _order(n, axis):
    bits = _bits(n)
    size, high = RING_HIGH.get(axis, (0, 0))
    if n == size and axis == "dp":
        bits = [high] + [k for k in bits if k != high]
    return bits


def _bits(n):
    bits = []
    k = 1
    while k < n:
        bits.append(k)
        k *= 2
    return bits


def tree_sum(x, axis):
    n = lax.axis_size(axis)
    for k in _bits(n):
        x = x + lax.ppermute(x, axis, _pairs(n, k, axis))
    return x


def flat_sum(x, axis):
    n = lax.axis_size(axis)
    idx = lax.axis_index(axis)
    got = [x] + [lax.ppermute(x, axis, [(i, (i + s) % n) for i in range(n)]) for s in range(1, n)]
    by_source = jnp.take(jnp.stack(got), (idx - jnp.arange(n)) % n, axis=0)
    return jnp.sum(by_source, axis=0)


def ring_sum(x, axis, halvings=1, tiny=None):
    n = lax.axis_size(axis)
    idx = lax.axis_index(axis)
    bits = _order(n, axis)
    split, whole = bits[:halvings], bits[halvings:]

    def add(x, tiny, perm):
        if tiny is None:
            return x + lax.ppermute(x, axis, perm), None
        got, got_tiny = lax.ppermute((x, tiny), axis, perm)
        return x + got, tiny + got_tiny

    for k in split:
        half = x.shape[0] // 2
        upper = (idx // k) % 2 == 1
        lo, hi = x[:half], x[half:]
        keep = jnp.where(upper, hi, lo)
        send = jnp.where(upper, lo, hi)
        if tiny is None:
            x = keep + lax.ppermute(send, axis, _pairs(n, k, axis))
        else:
            got, got_tiny = lax.ppermute((send, tiny), axis, _pairs(n, k, axis))
            x, tiny = keep + got, tiny + got_tiny
    if axis == "lm" and n == RING_HIGH["lm"][0] and split == [1]:
        second = whole[1:] + whole[:1]
        for step in range(len(whole)):
            mine = dict(_pairs(n, whole[step], axis))
            theirs = dict(_pairs(n, second[step], axis))
            x, tiny = add(x, tiny, [(i, mine[i] if i % 2 == 0 else theirs[i]) for i in range(n)])
    else:
        for k in whole:
            x, tiny = add(x, tiny, _pairs(n, k, axis))
    for k in reversed(split):
        upper = (idx // k) % 2 == 1
        other = lax.ppermute(x, axis, _pairs(n, k, axis))
        x = jnp.where(upper, jnp.concatenate([other, x], 0), jnp.concatenate([x, other], 0))
    if tiny is None:
        return x
    return x, tiny


def _dp_partner(d, k):
    if k == RING_HIGH["dp"][1]:
        lo = k // 2
        return d + (3 - 2 * ((d // lo) % 4)) * lo
    return d ^ k


def dp_sum(x):
    n_dp = lax.axis_size("dp")
    n_lm = lax.axis_size("lm")
    if n_dp != RING_HIGH["dp"][0] or n_lm % 2:
        return ring_sum(x, "dp")
    orders = ([2, 1, 4], [4, 2, 1])
    d = lax.axis_index("dp")
    second = lax.axis_index("lm") % 2 == 1

    def perm(step):
        return [
            (g, _dp_partner(g // n_lm, orders[(g % n_lm) % 2][step]) * n_lm + g % n_lm)
            for g in range(n_dp * n_lm)
        ]

    upper = jnp.where(second, (d // orders[1][0]) % 2 == 1, (d // orders[0][0]) % 2 == 1)
    half = x.shape[0] // 2
    lo, hi = x[:half], x[half:]
    keep = jnp.where(upper, hi, lo)
    send = jnp.where(upper, lo, hi)
    x = keep + lax.ppermute(send, ("dp", "lm"), perm(0))
    for step in range(1, len(orders[0])):
        x = x + lax.ppermute(x, ("dp", "lm"), perm(step))
    other = lax.ppermute(x, ("dp", "lm"), perm(0))
    return jnp.where(upper, jnp.concatenate([other, x], 0), jnp.concatenate([x, other], 0))


def gather_rows(x, axis):
    n = lax.axis_size(axis)
    idx = lax.axis_index(axis)
    bits = _bits(n)
    if not (axis == "lm" and n == RING_HIGH["lm"][0]):
        for k in bits:
            upper = (idx // k) % 2 == 1
            other = lax.ppermute(x, axis, _pairs(n, k, axis))
            x = jnp.where(upper, jnp.concatenate([other, x], 0), jnp.concatenate([x, other], 0))
        return x
    first = bits
    second = bits[:1] + bits[2:] + bits[1:2]
    block = x.shape[0]
    on_second = idx % 2 == 1
    for step in range(len(bits)):
        mine = dict(_pairs(n, first[step], axis))
        theirs = dict(_pairs(n, second[step], axis))
        perm = [(i, mine[i] if i % 2 == 0 else theirs[i]) for i in range(n)]
        upper = jnp.where(on_second, (idx // second[step]) % 2 == 1, (idx // first[step]) % 2 == 1)
        other = lax.ppermute(x, axis, perm)
        x = jnp.where(upper, jnp.concatenate([other, x], 0), jnp.concatenate([x, other], 0))

    def place(i):
        return sum(((i // k) % 2) << p for p, k in enumerate(second))

    ordered = jnp.concatenate([x[place(i) * block:(place(i) + 1) * block] for i in range(n)], 0)
    return jnp.where(on_second, ordered, x)


def shards(queries, landmarks, targets, ridge):
    qhat = normalize(gather_rows(queries.T, "lm").T)
    chat = normalize(landmarks)
    rows_dev = qhat.shape[0]
    lm_rows = chat.shape[0]
    width = qhat.shape[1]
    n_tg = targets.shape[1]
    block_rows = min(512, rows_dev)
    total_rows = float(rows_dev * lax.axis_size("dp"))
    first_dp = lax.axis_index("dp") == 0

    def tile_rows(block):
        scores = jnp.dot(block, chat.T, preferred_element_type=jnp.float32)
        tile = jnp.exp(2.0 * sharpness * scores).astype(jnp.bfloat16)
        values = tile.astype(jnp.float32)
        return (tile, jnp.sum(values * values, axis=0))

    tiles, column_sq = lax.map(tile_rows, qhat.reshape(rows_dev // block_rows, block_rows, width))
    kernel = tiles.reshape(rows_dev, lm_rows)
    rhs_part, sq_part = lax.optimization_barrier((lax.dot_general(
        kernel, targets, (((0,), (0,)), ((), ())), preferred_element_type=jnp.float32
    ), jnp.sum(column_sq, axis=0)))
    stacked = dp_sum(jnp.concatenate([rhs_part, sq_part[:, None]], 1))
    rhs = stacked[:, :n_tg] / total_rows
    precond = stacked[:, n_tg:] / total_rows + ridge[None, :]
    coefficients = jnp.zeros_like(rhs)
    residual = rhs
    direction = residual / precond
    norm_part = jnp.sum(residual * direction, axis=0)
    norm_now = None
    for step in range(ITERS):
        rounded = lax.optimization_barrier(direction.astype(jnp.bfloat16))
        image_part = lax.optimization_barrier(jnp.dot(kernel, rounded, preferred_element_type=jnp.float32))
        if norm_now is None:
            query_image, norm_now = ring_sum(image_part.astype(jnp.bfloat16), "lm", tiny=norm_part)
        else:
            query_image = ring_sum(image_part.astype(jnp.bfloat16), "lm")
        back_part = lax.optimization_barrier(lax.dot_general(
            kernel,
            lax.optimization_barrier(query_image.astype(jnp.bfloat16)),
            (((0,), (0,)), ((), ())),
            preferred_element_type=jnp.float32,
        ))
        dot_part = jnp.sum(direction * back_part, axis=0) / total_rows + jnp.where(
            first_dp, ridge * jnp.sum(direction * direction, axis=0), 0.0
        )
        if step + 1 < ITERS:
            extra = jnp.zeros((lm_rows, 1), jnp.float32).at[:n_tg, 0].set(dot_part)
            summed = dp_sum(jnp.concatenate([back_part, extra], 1))
            back = summed[:, :n_tg]
            dot_all = flat_sum(summed[:n_tg, n_tg], "lm")
        else:
            back = ring_sum(back_part, "dp")
            dot_all = flat_sum(flat_sum(dot_part, "dp"), "lm")
        image = back / total_rows + ridge[None, :] * direction
        alpha = norm_now / dot_all
        coefficients = coefficients + alpha[None, :] * direction
        residual = residual - alpha[None, :] * image
        if step + 1 < ITERS:
            scaled = residual / precond
            norm_next = flat_sum(jnp.sum(residual * scaled, axis=0), "lm")
            direction = scaled + (norm_next / norm_now)[None, :] * direction
            norm_now = norm_next
    rounded_coef = lax.optimization_barrier(coefficients.astype(jnp.bfloat16))
    return ring_sum(jnp.dot(kernel, rounded_coef, preferred_element_type=jnp.float32), "lm")


def solution(mesh):
    return jax.shard_map(
        shards,
        mesh=mesh,
        in_specs=(P("dp", "lm"), P("lm", None), P("dp", None), P()),
        out_specs=P("dp", None),
        check_vma=False,
    )
```

```python
import jax
import jax.numpy as jnp
from jax import lax
from jax.sharding import PartitionSpec as P

ITERS = 2


sharpness = 8.0
epsilon = 1e-06


def normalize(rows):
    values = rows.astype(jnp.float32)
    scale = lax.rsqrt(jnp.sum(values * values, axis=1, keepdims=True) + epsilon)
    return (values * scale).astype(jnp.bfloat16)


RING_HIGH = {"dp": (8, 2), "lm": (16, 8)}


def _pairs(n, k, axis=None):
    size, high = RING_HIGH.get(axis, (0, 0))
    if n == size and k == high:
        lo = k // 2
        return [(i, i + (3 - 2 * ((i // lo) % 4)) * lo) for i in range(n)]
    return [(i, i ^ k) for i in range(n)]


def _order(n, axis):
    bits = _bits(n)
    size, high = RING_HIGH.get(axis, (0, 0))
    if n == size and axis == "dp":
        bits = [high] + [k for k in bits if k != high]
    return bits


def _bits(n):
    bits = []
    k = 1
    while k < n:
        bits.append(k)
        k *= 2
    return bits


def tree_sum(x, axis):
    n = lax.axis_size(axis)
    for k in _bits(n):
        x = x + lax.ppermute(x, axis, _pairs(n, k, axis))
    return x


def ring_sum(x, axis, halvings=1, tiny=None):
    n = lax.axis_size(axis)
    idx = lax.axis_index(axis)
    bits = _order(n, axis)
    split, whole = bits[:halvings], bits[halvings:]

    def add(x, tiny, perm):
        if tiny is None:
            return x + lax.ppermute(x, axis, perm), None
        got, got_tiny = lax.ppermute((x, tiny), axis, perm)
        return x + got, tiny + got_tiny

    for k in split:
        half = x.shape[0] // 2
        upper = (idx // k) % 2 == 1
        lo, hi = x[:half], x[half:]
        keep = jnp.where(upper, hi, lo)
        send = jnp.where(upper, lo, hi)
        if tiny is None:
            x = keep + lax.ppermute(send, axis, _pairs(n, k, axis))
        else:
            got, got_tiny = lax.ppermute((send, tiny), axis, _pairs(n, k, axis))
            x, tiny = keep + got, tiny + got_tiny
    if axis == "lm" and n == RING_HIGH["lm"][0] and split == [1]:
        second = whole[1:] + whole[:1]
        for step in range(len(whole)):
            mine = dict(_pairs(n, whole[step], axis))
            theirs = dict(_pairs(n, second[step], axis))
            x, tiny = add(x, tiny, [(i, mine[i] if i % 2 == 0 else theirs[i]) for i in range(n)])
    else:
        for k in whole:
            x, tiny = add(x, tiny, _pairs(n, k, axis))
    for k in reversed(split):
        upper = (idx // k) % 2 == 1
        other = lax.ppermute(x, axis, _pairs(n, k, axis))
        x = jnp.where(upper, jnp.concatenate([other, x], 0), jnp.concatenate([x, other], 0))
    if tiny is None:
        return x
    return x, tiny


def _dp_partner(d, k):
    if k == RING_HIGH["dp"][1]:
        lo = k // 2
        return d + (3 - 2 * ((d // lo) % 4)) * lo
    return d ^ k


def dp_sum(x):
    n_dp = lax.axis_size("dp")
    n_lm = lax.axis_size("lm")
    if n_dp != RING_HIGH["dp"][0] or n_lm % 2:
        return ring_sum(x, "dp")
    orders = ([2, 1, 4], [4, 2, 1])
    d = lax.axis_index("dp")
    second = lax.axis_index("lm") % 2 == 1

    def perm(step):
        return [
            (g, _dp_partner(g // n_lm, orders[(g % n_lm) % 2][step]) * n_lm + g % n_lm)
            for g in range(n_dp * n_lm)
        ]

    upper = jnp.where(second, (d // orders[1][0]) % 2 == 1, (d // orders[0][0]) % 2 == 1)
    half = x.shape[0] // 2
    lo, hi = x[:half], x[half:]
    keep = jnp.where(upper, hi, lo)
    send = jnp.where(upper, lo, hi)
    x = keep + lax.ppermute(send, ("dp", "lm"), perm(0))
    for step in range(1, len(orders[0])):
        x = x + lax.ppermute(x, ("dp", "lm"), perm(step))
    other = lax.ppermute(x, ("dp", "lm"), perm(0))
    return jnp.where(upper, jnp.concatenate([other, x], 0), jnp.concatenate([x, other], 0))


def gather_rows(x, axis):
    n = lax.axis_size(axis)
    idx = lax.axis_index(axis)
    bits = _bits(n)
    if not (axis == "lm" and n == RING_HIGH["lm"][0]):
        for k in bits:
            upper = (idx // k) % 2 == 1
            other = lax.ppermute(x, axis, _pairs(n, k, axis))
            x = jnp.where(upper, jnp.concatenate([other, x], 0), jnp.concatenate([x, other], 0))
        return x
    first = bits
    second = bits[:1] + bits[2:] + bits[1:2]
    block = x.shape[0]
    on_second = idx % 2 == 1
    for step in range(len(bits)):
        mine = dict(_pairs(n, first[step], axis))
        theirs = dict(_pairs(n, second[step], axis))
        perm = [(i, mine[i] if i % 2 == 0 else theirs[i]) for i in range(n)]
        upper = jnp.where(on_second, (idx // second[step]) % 2 == 1, (idx // first[step]) % 2 == 1)
        other = lax.ppermute(x, axis, perm)
        x = jnp.where(upper, jnp.concatenate([other, x], 0), jnp.concatenate([x, other], 0))

    def place(i):
        return sum(((i // k) % 2) << p for p, k in enumerate(second))

    ordered = jnp.concatenate([x[place(i) * block:(place(i) + 1) * block] for i in range(n)], 0)
    return jnp.where(on_second, ordered, x)


def shards(queries, landmarks, targets, ridge):
    qhat = normalize(gather_rows(queries.T, "lm").T)
    chat = normalize(landmarks)
    rows_dev = qhat.shape[0]
    lm_rows = chat.shape[0]
    width = qhat.shape[1]
    n_tg = targets.shape[1]
    block_rows = rows_dev
    total_rows = float(rows_dev * lax.axis_size("dp"))
    first_dp = lax.axis_index("dp") == 0

    def tile_rows(block):
        scores = jnp.dot(block, chat.T, preferred_element_type=jnp.float32)
        tile = jnp.exp(2.0 * sharpness * scores).astype(jnp.bfloat16)
        values = tile.astype(jnp.float32)
        return (tile, jnp.sum(values * values, axis=0))

    tiles, column_sq = lax.map(tile_rows, qhat.reshape(rows_dev // block_rows, block_rows, width))
    kernel = tiles.reshape(rows_dev, lm_rows)
    rhs_part, sq_part = lax.optimization_barrier((lax.dot_general(
        kernel, targets, (((0,), (0,)), ((), ())), preferred_element_type=jnp.float32
    ), jnp.sum(column_sq, axis=0)))
    stacked = dp_sum(jnp.concatenate([rhs_part, sq_part[:, None]], 1))
    rhs = stacked[:, :n_tg] / total_rows
    precond = stacked[:, n_tg:] / total_rows + ridge[None, :]
    coefficients = jnp.zeros_like(rhs)
    residual = rhs
    direction = residual / precond
    norm_part = jnp.sum(residual * direction, axis=0)
    norm_now = None
    for step in range(ITERS):
        rounded = lax.optimization_barrier(direction.astype(jnp.bfloat16))
        image_part = lax.optimization_barrier(jnp.dot(kernel, rounded, preferred_element_type=jnp.float32))
        if norm_now is None:
            query_image, norm_now = ring_sum(image_part.astype(jnp.bfloat16), "lm", tiny=norm_part)
        else:
            query_image = ring_sum(image_part.astype(jnp.bfloat16), "lm")
        back_part = lax.optimization_barrier(lax.dot_general(
            kernel,
            lax.optimization_barrier(query_image.astype(jnp.bfloat16)),
            (((0,), (0,)), ((), ())),
            preferred_element_type=jnp.float32,
        ))
        dot_part = jnp.sum(direction * back_part, axis=0) / total_rows + jnp.where(
            first_dp, ridge * jnp.sum(direction * direction, axis=0), 0.0
        )
        if step + 1 < ITERS:
            extra = jnp.zeros((lm_rows, 1), jnp.float32).at[:n_tg, 0].set(dot_part)
            summed = dp_sum(jnp.concatenate([back_part, extra], 1))
            back = summed[:, :n_tg]
            dot_all = tree_sum(summed[:n_tg, n_tg], "lm")
        else:
            back = ring_sum(back_part, "dp")
            dot_all = tree_sum(tree_sum(dot_part, "dp"), "lm")
        image = back / total_rows + ridge[None, :] * direction
        alpha = norm_now / dot_all
        coefficients = coefficients + alpha[None, :] * direction
        residual = residual - alpha[None, :] * image
        if step + 1 < ITERS:
            scaled = residual / precond
            norm_next = tree_sum(jnp.sum(residual * scaled, axis=0), "lm")
            direction = scaled + (norm_next / norm_now)[None, :] * direction
            norm_now = norm_next
    rounded_coef = lax.optimization_barrier(coefficients.astype(jnp.bfloat16))
    return ring_sum(jnp.dot(kernel, rounded_coef, preferred_element_type=jnp.float32), "lm")


def solution(mesh):
    return jax.shard_map(
        shards,
        mesh=mesh,
        in_specs=(P("dp", "lm"), P("lm", None), P("dp", None), P()),
        out_specs=P("dp", None),
        check_vma=False,
    )
```

```python
import jax
import jax.numpy as jnp
from jax import lax
from jax.sharding import PartitionSpec as P

ITERS = 2


sharpness = 8.0
epsilon = 1e-06


def normalize(rows):
    values = rows.astype(jnp.float32)
    scale = lax.rsqrt(jnp.sum(values * values, axis=1, keepdims=True) + epsilon)
    return (values * scale).astype(jnp.bfloat16)


RING_HIGH = {"dp": (8, 2), "lm": (16, 8)}


def _pairs(n, k, axis=None):
    size, high = RING_HIGH.get(axis, (0, 0))
    if n == size and k == high:
        lo = k // 2
        return [(i, i + (3 - 2 * ((i // lo) % 4)) * lo) for i in range(n)]
    return [(i, i ^ k) for i in range(n)]


def _order(n, axis):
    bits = _bits(n)
    size, high = RING_HIGH.get(axis, (0, 0))
    if n == size and axis == "dp":
        bits = [high] + [k for k in bits if k != high]
    return bits


def _bits(n):
    bits = []
    k = 1
    while k < n:
        bits.append(k)
        k *= 2
    return bits


def tree_sum(x, axis):
    n = lax.axis_size(axis)
    for k in _bits(n):
        x = x + lax.ppermute(x, axis, _pairs(n, k, axis))
    return x


def ring_sum(x, axis, halvings=1, tiny=None):
    n = lax.axis_size(axis)
    idx = lax.axis_index(axis)
    bits = _order(n, axis)
    split, whole = bits[:halvings], bits[halvings:]

    def add(x, tiny, perm):
        if tiny is None:
            return x + lax.ppermute(x, axis, perm), None
        got, got_tiny = lax.ppermute((x, tiny), axis, perm)
        return x + got, tiny + got_tiny

    for k in split:
        half = x.shape[0] // 2
        upper = (idx // k) % 2 == 1
        lo, hi = x[:half], x[half:]
        keep = jnp.where(upper, hi, lo)
        send = jnp.where(upper, lo, hi)
        if tiny is None:
            x = keep + lax.ppermute(send, axis, _pairs(n, k, axis))
        else:
            got, got_tiny = lax.ppermute((send, tiny), axis, _pairs(n, k, axis))
            x, tiny = keep + got, tiny + got_tiny
    if axis == "lm" and n == RING_HIGH["lm"][0] and split == [1]:
        second = whole[1:] + whole[:1]
        for step in range(len(whole)):
            mine = dict(_pairs(n, whole[step], axis))
            theirs = dict(_pairs(n, second[step], axis))
            x, tiny = add(x, tiny, [(i, mine[i] if i % 2 == 0 else theirs[i]) for i in range(n)])
    else:
        for k in whole:
            x, tiny = add(x, tiny, _pairs(n, k, axis))
    for k in reversed(split):
        upper = (idx // k) % 2 == 1
        other = lax.ppermute(x, axis, _pairs(n, k, axis))
        x = jnp.where(upper, jnp.concatenate([other, x], 0), jnp.concatenate([x, other], 0))
    if tiny is None:
        return x
    return x, tiny


def _dp_partner(d, k):
    if k == RING_HIGH["dp"][1]:
        lo = k // 2
        return d + (3 - 2 * ((d // lo) % 4)) * lo
    return d ^ k


def dp_sum(x, tiny=None):
    n_dp = lax.axis_size("dp")
    n_lm = lax.axis_size("lm")
    if tiny is None:
        tiny = jnp.zeros((1,), x.dtype)
    if n_dp != RING_HIGH["dp"][0] or n_lm % 2:
        return ring_sum(x, "dp", tiny=tiny)
    orders = ([2, 1, 4], [4, 2, 1])
    d = lax.axis_index("dp")
    second = lax.axis_index("lm") % 2 == 1

    def perm(step):
        return [
            (g, _dp_partner(g // n_lm, orders[(g % n_lm) % 2][step]) * n_lm + g % n_lm)
            for g in range(n_dp * n_lm)
        ]

    upper = jnp.where(second, (d // orders[1][0]) % 2 == 1, (d // orders[0][0]) % 2 == 1)
    half = x.shape[0] // 2
    lo, hi = x[:half], x[half:]
    keep = jnp.where(upper, hi, lo)
    send = jnp.where(upper, lo, hi)
    got, got_tiny = lax.ppermute((send, tiny), ("dp", "lm"), perm(0))
    x, tiny = keep + got, tiny + got_tiny
    for step in range(1, len(orders[0])):
        got, got_tiny = lax.ppermute((x, tiny), ("dp", "lm"), perm(step))
        x, tiny = x + got, tiny + got_tiny
    other = lax.ppermute(x, ("dp", "lm"), perm(0))
    return jnp.where(upper, jnp.concatenate([other, x], 0), jnp.concatenate([x, other], 0)), tiny


def gather_rows(x, axis):
    n = lax.axis_size(axis)
    idx = lax.axis_index(axis)
    bits = _bits(n)
    if not (axis == "lm" and n == RING_HIGH["lm"][0]):
        for k in bits:
            upper = (idx // k) % 2 == 1
            other = lax.ppermute(x, axis, _pairs(n, k, axis))
            x = jnp.where(upper, jnp.concatenate([other, x], 0), jnp.concatenate([x, other], 0))
        return x
    first = bits
    second = bits[:1] + bits[2:] + bits[1:2]
    block = x.shape[0]
    on_second = idx % 2 == 1
    for step in range(len(bits)):
        mine = dict(_pairs(n, first[step], axis))
        theirs = dict(_pairs(n, second[step], axis))
        perm = [(i, mine[i] if i % 2 == 0 else theirs[i]) for i in range(n)]
        upper = jnp.where(on_second, (idx // second[step]) % 2 == 1, (idx // first[step]) % 2 == 1)
        other = lax.ppermute(x, axis, perm)
        x = jnp.where(upper, jnp.concatenate([other, x], 0), jnp.concatenate([x, other], 0))

    def place(i):
        return sum(((i // k) % 2) << p for p, k in enumerate(second))

    ordered = jnp.concatenate([x[place(i) * block:(place(i) + 1) * block] for i in range(n)], 0)
    return jnp.where(on_second, ordered, x)


def shards(queries, landmarks, targets, ridge):
    qhat = normalize(gather_rows(queries.T, "lm").T)
    chat = normalize(landmarks)
    rows_dev = qhat.shape[0]
    lm_rows = chat.shape[0]
    width = qhat.shape[1]
    n_tg = targets.shape[1]
    block_rows = rows_dev
    total_rows = float(rows_dev * lax.axis_size("dp"))
    first_dp = lax.axis_index("dp") == 0

    def tile_rows(block):
        scores = jnp.dot(block, chat.T, preferred_element_type=jnp.float32)
        tile = jnp.exp(2.0 * sharpness * scores).astype(jnp.bfloat16)
        values = tile.astype(jnp.float32)
        return (tile, jnp.sum(values * values, axis=0))

    tiles, column_sq = lax.map(tile_rows, qhat.reshape(rows_dev // block_rows, block_rows, width))
    kernel = tiles.reshape(rows_dev, lm_rows)
    rhs_part, sq_part = lax.optimization_barrier((lax.dot_general(
        kernel, targets, (((0,), (0,)), ((), ())), preferred_element_type=jnp.float32
    ), jnp.sum(column_sq, axis=0)))
    stacked, _ = dp_sum(jnp.concatenate([rhs_part, sq_part[:, None]], 1))
    rhs = stacked[:, :n_tg] / total_rows
    precond = stacked[:, n_tg:] / total_rows + ridge[None, :]
    coefficients = jnp.zeros_like(rhs)
    residual = rhs
    direction = residual / precond
    norm_part = jnp.sum(residual * direction, axis=0)
    norm_now = None
    for step in range(ITERS):
        rounded = lax.optimization_barrier(direction.astype(jnp.bfloat16))
        image_part = lax.optimization_barrier(jnp.dot(kernel, rounded, preferred_element_type=jnp.float32))
        if norm_now is None:
            query_image, norm_now = ring_sum(image_part.astype(jnp.bfloat16), "lm", tiny=norm_part)
        else:
            query_image = ring_sum(image_part.astype(jnp.bfloat16), "lm")
        back_part = lax.optimization_barrier(lax.dot_general(
            kernel,
            lax.optimization_barrier(query_image.astype(jnp.bfloat16)),
            (((0,), (0,)), ((), ())),
            preferred_element_type=jnp.float32,
        ))
        dot_part = jnp.sum(direction * back_part, axis=0) / total_rows + jnp.where(
            first_dp, ridge * jnp.sum(direction * direction, axis=0), 0.0
        )
        if step + 1 < ITERS:
            back, dot_dp = dp_sum(back_part, tiny=dot_part)
            dot_all = tree_sum(dot_dp, "lm")
        else:
            back = ring_sum(back_part, "dp")
            dot_all = tree_sum(tree_sum(dot_part, "dp"), "lm")
        image = back / total_rows + ridge[None, :] * direction
        alpha = norm_now / dot_all
        coefficients = coefficients + alpha[None, :] * direction
        residual = residual - alpha[None, :] * image
        if step + 1 < ITERS:
            scaled = residual / precond
            norm_next = tree_sum(jnp.sum(residual * scaled, axis=0), "lm")
            direction = scaled + (norm_next / norm_now)[None, :] * direction
            norm_now = norm_next
    rounded_coef = lax.optimization_barrier(coefficients.astype(jnp.bfloat16))
    return ring_sum(jnp.dot(kernel, rounded_coef, preferred_element_type=jnp.float32), "lm")


def solution(mesh):
    return jax.shard_map(
        shards,
        mesh=mesh,
        in_specs=(P("dp", "lm"), P("lm", None), P("dp", None), P()),
        out_specs=P("dp", None),
        check_vma=False,
    )
```

```python
import jax
import jax.numpy as jnp
from jax import lax
from jax.sharding import PartitionSpec as P

ITERS = 2


sharpness = 8.0
epsilon = 1e-06


def normalize(rows):
    values = rows.astype(jnp.float32)
    scale = lax.rsqrt(jnp.sum(values * values, axis=1, keepdims=True) + epsilon)
    return (values * scale).astype(jnp.bfloat16)


RING_HIGH = {"dp": (8, 2), "lm": (16, 8)}


def _pairs(n, k, axis=None):
    size, high = RING_HIGH.get(axis, (0, 0))
    if n == size and k == high:
        lo = k // 2
        return [(i, i + (3 - 2 * ((i // lo) % 4)) * lo) for i in range(n)]
    return [(i, i ^ k) for i in range(n)]


def _order(n, axis):
    bits = _bits(n)
    size, high = RING_HIGH.get(axis, (0, 0))
    if n == size and axis == "dp":
        bits = [high] + [k for k in bits if k != high]
    return bits


def _bits(n):
    bits = []
    k = 1
    while k < n:
        bits.append(k)
        k *= 2
    return bits


def tree_sum(x, axis):
    n = lax.axis_size(axis)
    for k in _bits(n):
        x = x + lax.ppermute(x, axis, _pairs(n, k, axis))
    return x


def ring_sum(x, axis, halvings=1, tiny=None):
    n = lax.axis_size(axis)
    idx = lax.axis_index(axis)
    bits = _order(n, axis)
    split, whole = bits[:halvings], bits[halvings:]

    def add(x, tiny, perm):
        if tiny is None:
            return x + lax.ppermute(x, axis, perm), None
        got, got_tiny = lax.ppermute((x, tiny), axis, perm)
        return x + got, tiny + got_tiny

    for k in split:
        half = x.shape[0] // 2
        upper = (idx // k) % 2 == 1
        lo, hi = x[:half], x[half:]
        keep = jnp.where(upper, hi, lo)
        send = jnp.where(upper, lo, hi)
        if tiny is None:
            x = keep + lax.ppermute(send, axis, _pairs(n, k, axis))
        else:
            got, got_tiny = lax.ppermute((send, tiny), axis, _pairs(n, k, axis))
            x, tiny = keep + got, tiny + got_tiny
    if axis == "lm" and n == RING_HIGH["lm"][0] and split == [1]:
        second = whole[1:] + whole[:1]
        for step in range(len(whole)):
            mine = dict(_pairs(n, whole[step], axis))
            theirs = dict(_pairs(n, second[step], axis))
            x, tiny = add(x, tiny, [(i, mine[i] if i % 2 == 0 else theirs[i]) for i in range(n)])
    else:
        for k in whole:
            x, tiny = add(x, tiny, _pairs(n, k, axis))
    for k in reversed(split):
        upper = (idx // k) % 2 == 1
        other = lax.ppermute(x, axis, _pairs(n, k, axis))
        x = jnp.where(upper, jnp.concatenate([other, x], 0), jnp.concatenate([x, other], 0))
    if tiny is None:
        return x
    return x, tiny


def _dp_partner(d, k):
    if k == RING_HIGH["dp"][1]:
        lo = k // 2
        return d + (3 - 2 * ((d // lo) % 4)) * lo
    return d ^ k


def dp_sum(x):
    n_dp = lax.axis_size("dp")
    n_lm = lax.axis_size("lm")
    if n_dp != RING_HIGH["dp"][0] or n_lm % 2:
        return jax.tree.map(lambda a: ring_sum(a, "dp"), x)
    orders = ([2, 1, 4], [4, 2, 1])
    d = lax.axis_index("dp")
    second = lax.axis_index("lm") % 2 == 1

    def perm(step):
        return [
            (g, _dp_partner(g // n_lm, orders[(g % n_lm) % 2][step]) * n_lm + g % n_lm)
            for g in range(n_dp * n_lm)
        ]

    upper = jnp.where(second, (d // orders[1][0]) % 2 == 1, (d // orders[0][0]) % 2 == 1)

    def keep(a):
        half = a.shape[0] // 2
        return jnp.where(upper, a[half:], a[:half])

    def send(a):
        half = a.shape[0] // 2
        return jnp.where(upper, a[:half], a[half:])

    got = lax.ppermute(jax.tree.map(send, x), ("dp", "lm"), perm(0))
    x = jax.tree.map(lambda a, b: keep(a) + b, x, got)
    for step in range(1, len(orders[0])):
        got = lax.ppermute(x, ("dp", "lm"), perm(step))
        x = jax.tree.map(lambda a, b: a + b, x, got)
    other = lax.ppermute(x, ("dp", "lm"), perm(0))
    return jax.tree.map(
        lambda a, b: jnp.where(upper, jnp.concatenate([b, a], 0), jnp.concatenate([a, b], 0)), x, other
    )


def gather_rows(x, axis):
    n = lax.axis_size(axis)
    idx = lax.axis_index(axis)
    bits = _bits(n)
    if not (axis == "lm" and n == RING_HIGH["lm"][0]):
        for k in bits:
            upper = (idx // k) % 2 == 1
            other = lax.ppermute(x, axis, _pairs(n, k, axis))
            x = jnp.where(upper, jnp.concatenate([other, x], 0), jnp.concatenate([x, other], 0))
        return x
    first = bits
    second = bits[:1] + bits[2:] + bits[1:2]
    block = x.shape[0]
    on_second = idx % 2 == 1
    for step in range(len(bits)):
        mine = dict(_pairs(n, first[step], axis))
        theirs = dict(_pairs(n, second[step], axis))
        perm = [(i, mine[i] if i % 2 == 0 else theirs[i]) for i in range(n)]
        upper = jnp.where(on_second, (idx // second[step]) % 2 == 1, (idx // first[step]) % 2 == 1)
        other = lax.ppermute(x, axis, perm)
        x = jnp.where(upper, jnp.concatenate([other, x], 0), jnp.concatenate([x, other], 0))

    def place(i):
        return sum(((i // k) % 2) << p for p, k in enumerate(second))

    ordered = jnp.concatenate([x[place(i) * block:(place(i) + 1) * block] for i in range(n)], 0)
    return jnp.where(on_second, ordered, x)


def shards(queries, landmarks, targets, ridge):
    qhat = normalize(gather_rows(queries.T, "lm").T)
    chat = normalize(landmarks)
    rows_dev = qhat.shape[0]
    lm_rows = chat.shape[0]
    width = qhat.shape[1]
    n_tg = targets.shape[1]
    block_rows = rows_dev
    total_rows = float(rows_dev * lax.axis_size("dp"))
    first_dp = lax.axis_index("dp") == 0

    def tile_rows(block):
        scores = jnp.dot(block, chat.T, preferred_element_type=jnp.float32)
        tile = jnp.exp(2.0 * sharpness * scores).astype(jnp.bfloat16)
        values = tile.astype(jnp.float32)
        return (tile, jnp.sum(values * values, axis=0))

    tiles, column_sq = lax.map(tile_rows, qhat.reshape(rows_dev // block_rows, block_rows, width))
    kernel = tiles.reshape(rows_dev, lm_rows)
    rhs_part, sq_part = lax.optimization_barrier((lax.dot_general(
        kernel, targets, (((0,), (0,)), ((), ())), preferred_element_type=jnp.float32
    ), jnp.sum(column_sq, axis=0)))
    rhs_sum, sq_sum = dp_sum((rhs_part, sq_part))
    rhs = rhs_sum / total_rows
    precond = sq_sum[:, None] / total_rows + ridge[None, :]
    coefficients = jnp.zeros_like(rhs)
    residual = rhs
    direction = residual / precond
    norm_part = jnp.sum(residual * direction, axis=0)
    norm_now = None
    for step in range(ITERS):
        rounded = lax.optimization_barrier(direction.astype(jnp.bfloat16))
        image_part = lax.optimization_barrier(jnp.dot(kernel, rounded, preferred_element_type=jnp.float32))
        if norm_now is None:
            query_image, norm_now = ring_sum(image_part.astype(jnp.bfloat16), "lm", tiny=norm_part)
        else:
            query_image = ring_sum(image_part.astype(jnp.bfloat16), "lm")
        back_part = lax.optimization_barrier(lax.dot_general(
            kernel,
            lax.optimization_barrier(query_image.astype(jnp.bfloat16)),
            (((0,), (0,)), ((), ())),
            preferred_element_type=jnp.float32,
        ))
        dot_part = jnp.sum(direction * back_part, axis=0) / total_rows + jnp.where(
            first_dp, ridge * jnp.sum(direction * direction, axis=0), 0.0
        )
        if step + 1 < ITERS:
            extra = jnp.zeros((lm_rows, 1), jnp.float32).at[:n_tg, 0].set(dot_part)
            summed = dp_sum(jnp.concatenate([back_part, extra], 1))
            back = summed[:, :n_tg]
            dot_all = tree_sum(summed[:n_tg, n_tg], "lm")
        else:
            back = ring_sum(back_part, "dp")
            dot_all = tree_sum(tree_sum(dot_part, "dp"), "lm")
        image = back / total_rows + ridge[None, :] * direction
        alpha = norm_now / dot_all
        coefficients = coefficients + alpha[None, :] * direction
        residual = residual - alpha[None, :] * image
        if step + 1 < ITERS:
            scaled = residual / precond
            norm_next = tree_sum(jnp.sum(residual * scaled, axis=0), "lm")
            direction = scaled + (norm_next / norm_now)[None, :] * direction
            norm_now = norm_next
    rounded_coef = lax.optimization_barrier(coefficients.astype(jnp.bfloat16))
    return ring_sum(jnp.dot(kernel, rounded_coef, preferred_element_type=jnp.float32), "lm")


def solution(mesh):
    return jax.shard_map(
        shards,
        mesh=mesh,
        in_specs=(P("dp", "lm"), P("lm", None), P("dp", None), P()),
        out_specs=P("dp", None),
        check_vma=False,
    )
```

```python
import jax
import jax.numpy as jnp
from jax import lax
from jax.sharding import PartitionSpec as P

ITERS = 2


sharpness = 8.0
epsilon = 1e-06


def normalize(rows):
    values = rows.astype(jnp.float32)
    scale = lax.rsqrt(jnp.sum(values * values, axis=1, keepdims=True) + epsilon)
    return (values * scale).astype(jnp.bfloat16)


RING_HIGH = {"dp": (8, 2), "lm": (16, 8)}


def _pairs(n, k, axis=None):
    size, high = RING_HIGH.get(axis, (0, 0))
    if n == size and k == high:
        lo = k // 2
        return [(i, i + (3 - 2 * ((i // lo) % 4)) * lo) for i in range(n)]
    return [(i, i ^ k) for i in range(n)]


def _order(n, axis):
    bits = _bits(n)
    size, high = RING_HIGH.get(axis, (0, 0))
    if n == size and axis == "dp":
        bits = [high] + [k for k in bits if k != high]
    return bits


def _bits(n):
    bits = []
    k = 1
    while k < n:
        bits.append(k)
        k *= 2
    return bits


def tree_sum(x, axis):
    n = lax.axis_size(axis)
    for k in _bits(n):
        x = x + lax.ppermute(x, axis, _pairs(n, k, axis))
    return x


def ring_sum(x, axis, halvings=1, tiny=None):
    n = lax.axis_size(axis)
    idx = lax.axis_index(axis)
    bits = _order(n, axis)
    split, whole = bits[:halvings], bits[halvings:]

    def add(x, tiny, perm):
        if tiny is None:
            return x + lax.ppermute(x, axis, perm), None
        got, got_tiny = lax.ppermute((x, tiny), axis, perm)
        return x + got, tiny + got_tiny

    for k in split:
        half = x.shape[0] // 2
        upper = (idx // k) % 2 == 1
        lo, hi = x[:half], x[half:]
        keep = jnp.where(upper, hi, lo)
        send = jnp.where(upper, lo, hi)
        if tiny is None:
            x = keep + lax.ppermute(send, axis, _pairs(n, k, axis))
        else:
            got, got_tiny = lax.ppermute((send, tiny), axis, _pairs(n, k, axis))
            x, tiny = keep + got, tiny + got_tiny
    if axis == "lm" and n == RING_HIGH["lm"][0] and split == [1]:
        second = whole[1:] + whole[:1]
        for step in range(len(whole)):
            mine = dict(_pairs(n, whole[step], axis))
            theirs = dict(_pairs(n, second[step], axis))
            x, tiny = add(x, tiny, [(i, mine[i] if i % 2 == 0 else theirs[i]) for i in range(n)])
    else:
        for k in whole:
            x, tiny = add(x, tiny, _pairs(n, k, axis))
    for k in reversed(split):
        upper = (idx // k) % 2 == 1
        other = lax.ppermute(x, axis, _pairs(n, k, axis))
        x = jnp.where(upper, jnp.concatenate([other, x], 0), jnp.concatenate([x, other], 0))
    if tiny is None:
        return x
    return x, tiny


def _dp_partner(d, k):
    if k == RING_HIGH["dp"][1]:
        lo = k // 2
        return d + (3 - 2 * ((d // lo) % 4)) * lo
    return d ^ k


def dp_sum(x):
    n_dp = lax.axis_size("dp")
    n_lm = lax.axis_size("lm")
    if n_dp != RING_HIGH["dp"][0] or n_lm % 2:
        return ring_sum(x, "dp")
    orders = ([2, 1, 4], [4, 2, 1])
    d = lax.axis_index("dp")
    second = lax.axis_index("lm") % 2 == 1

    def perm(step):
        return [
            (g, _dp_partner(g // n_lm, orders[(g % n_lm) % 2][step]) * n_lm + g % n_lm)
            for g in range(n_dp * n_lm)
        ]

    upper = jnp.where(second, (d // orders[1][0]) % 2 == 1, (d // orders[0][0]) % 2 == 1)
    half = x.shape[0] // 2
    lo, hi = x[:half], x[half:]
    keep = jnp.where(upper, hi, lo)
    send = jnp.where(upper, lo, hi)
    x = keep + lax.ppermute(send, ("dp", "lm"), perm(0))
    for step in range(1, len(orders[0])):
        x = x + lax.ppermute(x, ("dp", "lm"), perm(step))
    other = lax.ppermute(x, ("dp", "lm"), perm(0))
    return jnp.where(upper, jnp.concatenate([other, x], 0), jnp.concatenate([x, other], 0))


def gather_rows(x, axis):
    n = lax.axis_size(axis)
    idx = lax.axis_index(axis)
    bits = _bits(n)
    if not (axis == "lm" and n == RING_HIGH["lm"][0]):
        for k in bits:
            upper = (idx // k) % 2 == 1
            other = lax.ppermute(x, axis, _pairs(n, k, axis))
            x = jnp.where(upper, jnp.concatenate([other, x], 0), jnp.concatenate([x, other], 0))
        return x
    first = bits
    second = bits[:1] + bits[2:] + bits[1:2]
    block = x.shape[0]
    on_second = idx % 2 == 1
    for step in range(len(bits)):
        mine = dict(_pairs(n, first[step], axis))
        theirs = dict(_pairs(n, second[step], axis))
        perm = [(i, mine[i] if i % 2 == 0 else theirs[i]) for i in range(n)]
        upper = jnp.where(on_second, (idx // second[step]) % 2 == 1, (idx // first[step]) % 2 == 1)
        other = lax.ppermute(x, axis, perm)
        x = jnp.where(upper, jnp.concatenate([other, x], 0), jnp.concatenate([x, other], 0))

    def place(i):
        return sum(((i // k) % 2) << p for p, k in enumerate(second))

    ordered = jnp.concatenate([x[place(i) * block:(place(i) + 1) * block] for i in range(n)], 0)
    return jnp.where(on_second, ordered, x)


def shards(queries, landmarks, targets, ridge):
    qhat = normalize(gather_rows(queries.T, "lm").T)
    chat = normalize(landmarks)
    rows_dev = qhat.shape[0]
    lm_rows = chat.shape[0]
    width = qhat.shape[1]
    n_tg = targets.shape[1]
    block_rows = rows_dev
    total_rows = float(rows_dev * lax.axis_size("dp"))
    first_dp = lax.axis_index("dp") == 0

    def tile_rows(block):
        scores = jnp.dot(block, chat.T, preferred_element_type=jnp.float32)
        tile = jnp.exp(2.0 * sharpness * scores).astype(jnp.bfloat16)
        values = tile.astype(jnp.float32)
        return (tile, jnp.sum(values * values, axis=0))

    tiles, column_sq = lax.map(tile_rows, qhat.reshape(rows_dev // block_rows, block_rows, width))
    kernel = tiles.reshape(rows_dev, lm_rows)
    rhs_part, sq_part = lax.optimization_barrier((lax.dot_general(
        kernel, targets, (((0,), (0,)), ((), ())), preferred_element_type=jnp.float32
    ), jnp.sum(column_sq, axis=0)))
    stacked = dp_sum(jnp.concatenate([rhs_part, sq_part[:, None]], 1))
    rhs = stacked[:, :n_tg] / total_rows
    precond = stacked[:, n_tg:] / total_rows + ridge[None, :]
    coefficients = jnp.zeros_like(rhs)
    residual = rhs
    direction = residual / precond
    norm_part = jnp.sum(residual * direction, axis=0)
    norm_now = None
    for step in range(ITERS):
        rounded = lax.optimization_barrier(direction.astype(jnp.bfloat16))
        image_part = lax.optimization_barrier(jnp.dot(kernel, rounded, preferred_element_type=jnp.float32))
        query_image = ring_sum(image_part.astype(jnp.bfloat16), "lm")
        back_part = lax.optimization_barrier(lax.dot_general(
            kernel,
            lax.optimization_barrier(query_image.astype(jnp.bfloat16)),
            (((0,), (0,)), ((), ())),
            preferred_element_type=jnp.float32,
        ))
        dot_part = jnp.sum(direction * back_part, axis=0) / total_rows + jnp.where(
            first_dp, ridge * jnp.sum(direction * direction, axis=0), 0.0
        )
        if step + 1 < ITERS:
            extra = jnp.zeros((lm_rows, 1), jnp.float32).at[:n_tg, 0].set(dot_part)
            if norm_now is None:
                extra = extra.at[n_tg:2 * n_tg, 0].set(jnp.where(first_dp, norm_part, 0.0))
            summed = dp_sum(jnp.concatenate([back_part, extra], 1))
            back = summed[:, :n_tg]
            both = tree_sum(summed[:2 * n_tg, n_tg], "lm")
            dot_all = both[:n_tg]
            if norm_now is None:
                norm_now = both[n_tg:]
        else:
            back = ring_sum(back_part, "dp")
            dot_all = tree_sum(tree_sum(dot_part, "dp"), "lm")
            if norm_now is None:
                norm_now = tree_sum(norm_part, "lm")
        image = back / total_rows + ridge[None, :] * direction
        alpha = norm_now / dot_all
        coefficients = coefficients + alpha[None, :] * direction
        residual = residual - alpha[None, :] * image
        if step + 1 < ITERS:
            scaled = residual / precond
            norm_next = tree_sum(jnp.sum(residual * scaled, axis=0), "lm")
            direction = scaled + (norm_next / norm_now)[None, :] * direction
            norm_now = norm_next
    rounded_coef = lax.optimization_barrier(coefficients.astype(jnp.bfloat16))
    return ring_sum(jnp.dot(kernel, rounded_coef, preferred_element_type=jnp.float32), "lm")


def solution(mesh):
    return jax.shard_map(
        shards,
        mesh=mesh,
        in_specs=(P("dp", "lm"), P("lm", None), P("dp", None), P()),
        out_specs=P("dp", None),
        check_vma=False,
    )
```
